768 devices in a mesh: row: 16 (over y, core), col: 48 (over z, x).
Axes of the slice: x: 4, y: 8, z: 12, core: 2. Of those that a mesh axis runs over, the one named last changes fastest.
Arguments:
- matrix: float32 [4, 16, 48, 256, 256], P(None, 'row', 'col'), as said below
- present: int32 [4, 16, 48], P(None, 'row', 'col'), may hold values from 0 to 1, as said below
- update: int32 [2, 4, 16, 48], P(None, None, 'row', 'col'), may hold values from 0 to 1, as said below
Outputs:
- factored: float32 [4, 16, 48, 256, 256], P(None, 'row', 'col')
The draws below stay inside these ranges and needn't reach their ends.
Inputs may be any that keep to these rules, and one draw needn't show every extreme that they name: `present`: listed tiles lie on or below the diagonal (row >= column). Tiles (0, 0), (1, 0), (1, 1) and every diagonal tile (c, c) of the window, that is with c < 64 and c < 48, are listed; in column 1 every row i >= 1 whose tile in column 0 is listed is listed too. update[k, s, r, c] is 1 exactly where c > k and the tiles (i, c), (i, k) and (c, k) are all listed, with i = r + 16 s. `matrix`: unlisted tiles are zero. Tile (0, 0) is symmetric positive definite, and so is tile (1, 1) minus P0(1) P0(1)^T.
All inputs are finite; a program needn't handle non-finite values.
Results may differ from the reference program's by a relative error of at most 0.0001.
Values sent between devices are 32-bit elements; how exact they have to be, the bound alone decides.
No kernel may reach another device: no remote copies, remote signals or barrier semaphores. Data moves between devices by JAX's collectives and lax.ppermute only.
A program may use at most 32 MiB of HBM per device.

```python
import math
import jax
import jax.numpy as jnp
from jax import lax

B = 256
SLOTS = 4
N_ROW = 16
N_COL = 48


def tile_layout(base_key):
    structure_key = jax.random.fold_in(base_key, 101)
    tile_row = jnp.arange(SLOTS)[:, None, None] * N_ROW + jnp.arange(N_ROW)[None, :, None]
    tile_col = jnp.arange(N_COL)[None, None, :]
    coin_flip = jax.random.randint(structure_key, (SLOTS, N_ROW, N_COL), 0, 4)
    first_col = (tile_col == 0) & ((coin_flip < 3) | (tile_row <= 1))
    first_rows = first_col[:, :, 0]
    second = (tile_col == 1) & (tile_row >= 1) & (first_rows[:, :, None] | (coin_flip == 0))
    trailing = (tile_col >= 2) & (tile_row >= tile_col) & ((coin_flip < 2) | (tile_row == tile_col))
    listed = first_col | second | trailing
    updates = []
    for panel in range(2):
        along_col = listed[:, :, panel]
        top_rows = along_col.reshape(SLOTS * N_ROW)[:N_COL]
        if SLOTS * N_ROW < N_COL:
            top_rows = jnp.concatenate([top_rows, jnp.zeros((N_COL - SLOTS * N_ROW,), bool)])
        flag_set = listed & along_col[:, :, None] & top_rows[None, None, :] & (tile_col > panel)
        updates.append(flag_set)
    return (listed.astype(jnp.int32), jnp.stack(updates).astype(jnp.int32))


def draw_present(key, part):
    return tile_layout(key)[0]


def draw_update(key, part):
    return tile_layout(key)[1]


def draw_matrix(key, part):
    listed = tile_layout(key)[0]
    float_key = jax.random.fold_in(key, 202)
    first_key, second_key, third_key = jax.random.split(float_key, 3)
    shape = (SLOTS, N_ROW, N_COL, B, B)
    tile_row = (jnp.arange(SLOTS)[:, None, None] * N_ROW + jnp.arange(N_ROW)[None, :, None])[:, :, :, None, None]
    tile_col = jnp.arange(N_COL)[None, None, :, None, None]
    on_diag = jnp.arange(B)[:, None] == jnp.arange(B)[None, :]
    noise = jax.random.uniform(first_key, shape, jnp.float32, -1.0, 1.0)
    symmetric = 0.5 * (noise + jnp.swapaxes(noise, -1, -2))
    level = jax.random.uniform(second_key, shape, jnp.float32, 0.0, 1.0)
    diagonal_tile = jnp.where(on_diag, 4.0 * (1.0 + 0.5 * level), symmetric * (2.0 / math.sqrt(B)))
    coupling_tile = jnp.where(on_diag, 1.5 * (2.0 * level - 1.0), noise * (0.5 / B))
    general = jnp.clip(jax.random.normal(third_key, shape, jnp.float32), -6.0, 6.0)
    value = jnp.where(tile_row == tile_col, diagonal_tile, jnp.where((tile_row == 1) & (tile_col == 0), coupling_tile, jnp.where(tile_col <= 1, 0.25 * general, general)))
    return value * listed[:, :, :, None, None].astype(jnp.float32)


def setup_inputs(seed: int = 0) -> dict:
    splits = jax.random.split(jax.random.key(seed), 4)
    matrix = draw_matrix(jax.random.fold_in(splits[3], 71), 0)
    present = draw_present(jax.random.fold_in(splits[3], 71), 0)
    update = draw_update(jax.random.fold_in(splits[3], 71), 0)
    return dict(matrix=matrix, present=present, update=update)


def solve_panel(factor, blocks):
    count = blocks.shape[0]
    width = blocks.shape[-1]
    stacked = jnp.transpose(blocks, (2, 0, 1)).reshape(width, count * width)
    solved = jax.scipy.linalg.solve_triangular(factor, stacked, lower=True)
    return jnp.transpose(solved.reshape(width, count, width), (1, 2, 0))

def reference(matrix, present, update):
    slot_count = matrix.shape[0]
    row_count = matrix.shape[1]
    col_count = matrix.shape[2]
    width = matrix.shape[-1]
    tile_data = matrix
    for panel in range(2):
        factor = jnp.linalg.cholesky(tile_data[0, panel, panel])
        column = tile_data[:, :, panel].reshape(slot_count * row_count, width, width)
        solved = solve_panel(factor, column)
        solved = solved.at[panel].set(factor)
        far_tiles = solved[:col_count]
        if far_tiles.shape[0] < col_count:
            filler = jnp.zeros((col_count - far_tiles.shape[0], width, width), jnp.float32)
            far_tiles = jnp.concatenate([far_tiles, filler], 0)
        solved_grid = solved.reshape(slot_count, row_count, width, width)
        tile_data = tile_data.at[:, :, panel].set(solved_grid)
        pair_flags = update[panel].astype(jnp.float32)
        blocks = []
        for slot in range(slot_count):
            product = jnp.einsum('rab,cdb->rcad', solved_grid[slot], far_tiles, precision=lax.Precision.HIGHEST)
            blocks.append(tile_data[slot] - pair_flags[slot][:, :, None, None] * product)
        tile_data = jnp.stack(blocks)
    return tile_data * present.astype(jnp.float32)[:, :, :, None, None]
```

```python
import numpy as np
import jax
import jax.numpy as jnp
from jax import lax
from jax.sharding import Mesh
from jax.sharding import PartitionSpec as P

AXES = ("y", "core", "z", "x")
ROW = ("y", "core")
COL = ("z", "x")


def split_rounds(n, fan=2):
    spans = [(0, n)]
    rounds = []
    while any(length > 1 for _, length in spans):
        sends = [[] for _ in range(fan)]
        next_spans = []
        for start, length in spans:
            parts = min(fan + 1, length)
            sizes = [length // parts + (1 if i < length % parts else 0) for i in range(parts)]
            offset = start
            for i, size in enumerate(sizes):
                if i > 0:
                    sends[i - 1].append((start, offset))
                next_spans.append((offset, size))
                offset += size
        rounds.append([s for s in sends if s])
        spans = next_spans
    return rounds


class Grid:
    def __init__(self, shape):
        self.shape = shape
        ny, nk, nz, nx = shape
        self.n_row = ny * nk
        self.n_col = nz * nx
        self.y = lax.axis_index("y")
        self.core = lax.axis_index("core")
        self.z = lax.axis_index("z")
        self.x = lax.axis_index("x")
        self.row = self.y * nk + self.core
        self.col = self.z * nx + self.x
        self.lin = ((self.y * nk + self.core) * nz + self.z) * nx + self.x

    def index(self, y, k, z, x):
        ny, nk, nz, nx = self.shape
        return ((y * nk + k) * nz + z) * nx + x

    def send(self, value, pairs):
        perm = [(self.index(*s), self.index(*d)) for s, d in pairs]
        got = lax.ppermute(value, AXES, perm)
        mask = np.zeros(int(np.prod(self.shape)), bool)
        mask[[d for _, d in perm]] = True
        hit = jnp.asarray(mask)[self.lin]
        return got, hit

    def down_columns(self, value, roots):
        ny, nk, nz, nx = self.shape
        pairs = []
        for c, r in roots.items():
            z, x = divmod(c, nx)
            y0, k0 = divmod(r, nk)
            for k in range(nk):
                if k != k0:
                    pairs.append(((y0, k0, z, x), (y0, k, z, x)))
        if pairs:
            got, hit = self.send(value, pairs)
            value = jnp.where(hit, got, value)
        for sends in split_rounds(ny):
            results = []
            for offsets in sends:
                pairs = []
                for c, r in roots.items():
                    z, x = divmod(c, nx)
                    y0 = r // nk
                    for a, b in offsets:
                        for k in range(nk):
                            pairs.append((((y0 + a) % ny, k, z, x), ((y0 + b) % ny, k, z, x)))
                results.append(self.send(value, pairs))
            for got, hit in results:
                value = jnp.where(hit, got, value)
        return value

    def along_rows(self, tiles, root_col):
        ny, nk, nz, nx = self.shape
        slots = tiles.shape[0]
        z0, x0 = divmod(root_col, nx)
        rows = [(y, k) for y in range(ny) for k in range(nk)]
        assert slots == nx
        held = tiles[0]
        for j in range(1, nx):
            pairs = [((y, k, z0, x0), (y, k, z0, (x0 + j) % nx)) for y, k in rows]
            got, hit = self.send(tiles[j], pairs)
            held = jnp.where(hit, got, held)
        for sends in split_rounds(nz):
            results = []
            for offsets in sends:
                pairs = [
                    ((y, k, (z0 + a) % nz, x), (y, k, (z0 + b) % nz, x))
                    for y, k in rows
                    for x in range(nx)
                    for a, b in offsets
                ]
                results.append(self.send(held, pairs))
            for got, hit in results:
                held = jnp.where(hit, got, held)
        pieces = {0: held}
        left = held
        right = held
        for step in range(1, (nx - 1) // 2 + 2):
            if len(pieces) >= nx:
                break
            shift = [((y, k, z, x), (y, k, z, (x + 1) % nx)) for y, k in rows for z in range(nz) for x in range(nx)]
            left, _ = self.send(left, shift)
            pieces[-step] = left
            if len(pieces) >= nx:
                break
            shift = [((y, k, z, x), (y, k, z, (x - 1) % nx)) for y, k in rows for z in range(nz) for x in range(nx)]
            right, _ = self.send(right, shift)
            pieces[step] = right
        offsets = sorted(pieces)
        stack = jnp.stack([pieces[o] for o in offsets])
        base = (self.x - x0) % nx
        order = []
        for j in range(nx):
            pick = jnp.zeros((), jnp.int32)
            for i, o in enumerate(offsets):
                pick = jnp.where((base + o) % nx == j, i, pick)
            order.append(pick)
        return jnp.take(stack, jnp.stack(order), axis=0)


def solve_panel(factor, blocks):
    count = blocks.shape[0]
    width = blocks.shape[-1]
    stacked = jnp.transpose(blocks, (2, 0, 1)).reshape(width, count * width)
    solved = jax.scipy.linalg.solve_triangular(factor, stacked, lower=True)
    return jnp.transpose(solved.reshape(width, count, width), (1, 2, 0))


def products(rows, far):
    return jnp.einsum("sab,db->sad", rows, far, precision=lax.Precision.HIGHEST)


def make_on_device(shape):
    def on_device(matrix, present, update):
        g = Grid(shape)
        tiles = matrix[:, 0, 0]
        listed = present[:, 0, 0].astype(jnp.float32)
        flags = update[:, :, 0, 0].astype(jnp.float32)
        width = tiles.shape[-1]
        slots = tiles.shape[0]
        n_row, n_col = g.n_row, g.n_col
        identity = jnp.eye(width, dtype=jnp.float32)
        far_slot = g.col // n_row
        far_root = {c: c % n_row for c in range(n_col)}

        def panel_factor(work, k):
            owner = (g.row == k) & (g.col == k)
            factor = jnp.linalg.cholesky(jnp.where(owner, work[0], identity))
            factor = g.down_columns(factor, {k: k})
            solved = lax.cond(g.col == k, lambda d: solve_panel(factor, d), lambda d: d, work)
            return solved.at[0].set(jnp.where(owner, factor, solved[0]))

        p0 = panel_factor(tiles, 0)
        pairs = [((y, k, 0, 0), (y, k, 0, 1)) for y in range(shape[0]) for k in range(shape[1])]
        r01, _ = g.send(p0, pairs)
        f01 = g.down_columns(r01[1 // n_row], {1: 1 % n_row})
        work1 = tiles - flags[0][:, None, None] * products(r01, f01)
        p1 = panel_factor(work1, 1)

        r0 = g.along_rows(p0, 0)
        f0 = g.down_columns(lax.dynamic_index_in_dim(r0, far_slot, 0, keepdims=False), far_root)
        r1 = g.along_rows(p1, 1)
        f1 = g.down_columns(lax.dynamic_index_in_dim(r1, far_slot, 0, keepdims=False), far_root)
        rest = (tiles - flags[0][:, None, None] * products(r0, f0)) - flags[1][:, None, None] * products(r1, f1)
        out = jnp.where(g.col == 0, p0, jnp.where(g.col == 1, p1, rest))
        return (out * listed[:, None, None])[:, None, None]

    return on_device


def solution(mesh):
    n_row = mesh.shape["row"]
    n_col = mesh.shape["col"]
    shape = (n_row // 2, 2, n_col // 4, 4)
    finer = Mesh(mesh.devices.reshape(shape), AXES)
    return jax.shard_map(
        make_on_device(shape),
        mesh=finer,
        in_specs=(P(None, ROW, COL, None, None), P(None, ROW, COL), P(None, None, ROW, COL)),
        out_specs=P(None, ROW, COL, None, None),
        check_vma=False,
    )
```

```python
import numpy as np
import jax
import jax.numpy as jnp
from jax import lax
from jax.sharding import Mesh
from jax.sharding import PartitionSpec as P

AXES = ("y", "core", "z", "x")
ROW = ("y", "core")
COL = ("z", "x")


def split_rounds(n, fan=2):
    spans = [(0, n)]
    rounds = []
    while any(length > 1 for _, length in spans):
        sends = [[] for _ in range(fan)]
        next_spans = []
        for start, length in spans:
            parts = min(fan + 1, length)
            sizes = [length // parts + (1 if i < length % parts else 0) for i in range(parts)]
            offset = start
            for i, size in enumerate(sizes):
                if i > 0:
                    sends[i - 1].append((start, offset))
                next_spans.append((offset, size))
                offset += size
        rounds.append([s for s in sends if s])
        spans = next_spans
    return rounds


class Grid:
    def __init__(self, shape):
        self.shape = shape
        ny, nk, nz, nx = shape
        self.n_row = ny * nk
        self.n_col = nz * nx
        self.y = lax.axis_index("y")
        self.core = lax.axis_index("core")
        self.z = lax.axis_index("z")
        self.x = lax.axis_index("x")
        self.row = self.y * nk + self.core
        self.col = self.z * nx + self.x
        self.lin = ((self.y * nk + self.core) * nz + self.z) * nx + self.x

    def index(self, y, k, z, x):
        ny, nk, nz, nx = self.shape
        return ((y * nk + k) * nz + z) * nx + x

    def send(self, value, pairs):
        perm = [(self.index(*s), self.index(*d)) for s, d in pairs]
        got = lax.ppermute(value, AXES, perm)
        mask = np.zeros(int(np.prod(self.shape)), bool)
        mask[[d for _, d in perm]] = True
        hit = jnp.asarray(mask)[self.lin]
        return got, hit

    def down_columns(self, value, roots):
        ny, nk, nz, nx = self.shape
        pairs = []
        for c, r in roots.items():
            z, x = divmod(c, nx)
            y0, k0 = divmod(r, nk)
            for k in range(nk):
                if k != k0:
                    pairs.append(((y0, k0, z, x), (y0, k, z, x)))
        if pairs:
            got, hit = self.send(value, pairs)
            value = jnp.where(hit, got, value)
        for sends in split_rounds(ny):
            results = []
            for offsets in sends:
                pairs = []
                for c, r in roots.items():
                    z, x = divmod(c, nx)
                    y0 = r // nk
                    for a, b in offsets:
                        for k in range(nk):
                            pairs.append((((y0 + a) % ny, k, z, x), ((y0 + b) % ny, k, z, x)))
                results.append(self.send(value, pairs))
            for got, hit in results:
                value = jnp.where(hit, got, value)
        return value

    def along_rows(self, tiles, root_col, skip=()):
        ny, nk, nz, nx = self.shape
        slots = tiles.shape[0]
        assert slots == nx
        z0, x0 = divmod(root_col, nx)
        skipped = {divmod(c, nx) for c in skip}
        rows = [(y, k) for y in range(ny) for k in range(nk)]
        line_root = {x0: z0}
        held = tiles[0]
        for j in range(1, nx):
            x = (x0 + j) % nx
            z = z0
            while (z, x) in skipped:
                z = (z + 1) % nz
            line_root[x] = z
            pairs = [((y, k, z0, x0), (y, k, z, x)) for y, k in rows]
            got, hit = self.send(tiles[j], pairs)
            held = jnp.where(hit, got, held)
        trees = {}
        for x in range(nx):
            zs = [(line_root[x] + t) % nz for t in range(nz)]
            trees[x] = [z for z in zs if (z, x) not in skipped]
        depth = max(len(split_rounds(len(t))) for t in trees.values())
        plans = {x: split_rounds(len(t)) for x, t in trees.items()}
        for level in range(depth):
            fan = max(len(plans[x][level]) for x in plans if level < len(plans[x]))
            results = []
            for i in range(fan):
                pairs = []
                for x, plan in plans.items():
                    if level < len(plan) and i < len(plan[level]):
                        zs = trees[x]
                        for a, b in plan[level][i]:
                            pairs += [((y, k, zs[a], x), (y, k, zs[b], x)) for y, k in rows]
                if pairs:
                    results.append(self.send(held, pairs))
            for got, hit in results:
                held = jnp.where(hit, got, held)
        buffers = [held]
        table = np.zeros((int(np.prod(self.shape)), nx), np.int32)
        for d in range(1, nx):
            pairs = []
            for z in range(nz):
                for x in range(nx):
                    t = (x + d) % nx
                    if (z, x) in skipped or (z, t) in skipped or (z, t) == (z0, x0):
                        continue
                    pairs += [((y, k, z, x), (y, k, z, t)) for y, k in rows]
            if pairs:
                got, _ = self.send(held, pairs)
                buffers.append(got)
                for y, k in rows:
                    for z in range(nz):
                        for t in range(nx):
                            x = (t - d) % nx
                            if (z, x) not in skipped and (z, t) not in skipped:
                                table[self.index(y, k, z, t), (x - x0) % nx] = len(buffers) - 1
        for z, x in sorted(skipped):
            j = (x - x0) % nx
            for t in range(nx):
                if (z, t) in skipped or (z, t) == (z0, x0):
                    continue
                pairs = [((y, k, z0, x0), (y, k, z, t)) for y, k in rows]
                got, _ = self.send(tiles[j], pairs)
                buffers.append(got)
                for y, k in rows:
                    table[self.index(y, k, z, t), j] = len(buffers) - 1
        for y, k in rows:
            for z in range(nz):
                for x in range(nx):
                    table[self.index(y, k, z, x), (x - x0) % nx] = 0
        order = jnp.asarray(table)[self.lin]
        out = jnp.take(jnp.stack(buffers), order, axis=0)
        is_root = (self.z == z0) & (self.x == x0)
        return jnp.where(is_root, tiles, out)


def solve_panel(factor, blocks):
    count = blocks.shape[0]
    width = blocks.shape[-1]
    stacked = jnp.transpose(blocks, (2, 0, 1)).reshape(width, count * width)
    solved = jax.scipy.linalg.solve_triangular(factor, stacked, lower=True)
    return jnp.transpose(solved.reshape(width, count, width), (1, 2, 0))


def products(rows, far):
    return jnp.einsum("sab,db->sad", rows, far, precision=lax.Precision.HIGHEST)


def make_on_device(shape):
    def on_device(matrix, present, update):
        g = Grid(shape)
        tiles = matrix[:, 0, 0]
        listed = present[:, 0, 0].astype(jnp.float32)
        flags = update[:, :, 0, 0].astype(jnp.float32)
        width = tiles.shape[-1]
        n_row, n_col = g.n_row, g.n_col
        identity = jnp.eye(width, dtype=jnp.float32)
        far_slot = g.col // n_row
        far_root = {c: c % n_row for c in range(2, n_col)}

        def factor_on_owner(k, tile):
            owner = (g.row == k) & (g.col == k)
            factor = lax.cond(owner, jnp.linalg.cholesky, lambda t: identity, tile)
            return owner, g.down_columns(factor, {k: k})

        def solve_column(k, owner, factor, work):
            solved = lax.cond(g.col == k, lambda d: solve_panel(factor, d), lambda d: d, work)
            return solved.at[0].set(jnp.where(owner, factor, solved[0]))

        owner0, factor0 = factor_on_owner(0, tiles[0])
        p0 = solve_column(0, owner0, factor0, tiles)
        got, _ = g.send(p0[0], [((0, 1, 0, 0), (0, 1, 0, 1))])
        work11 = tiles[0] - flags[0, 0] * products(got[None], got)[0]
        f01 = g.down_columns(p0[0], {0: 1 % n_row})
        pairs = [((y, k, 0, 0), (y, k, 0, 1)) for y in range(shape[0]) for k in range(shape[1])]
        q01, _ = g.send(products(p0, f01), pairs)
        owner1, factor1 = factor_on_owner(1, work11)
        work1 = tiles - flags[0][:, None, None] * q01
        p1 = solve_column(1, owner1, factor1, work1)

        r0 = g.along_rows(p0, 0, skip=(1,))
        f0 = g.down_columns(lax.dynamic_index_in_dim(r0, far_slot, 0, keepdims=False), far_root)
        r1 = g.along_rows(p1, 1, skip=(0,))
        f1 = g.down_columns(lax.dynamic_index_in_dim(r1, far_slot, 0, keepdims=False), far_root)
        rest = (tiles - flags[0][:, None, None] * products(r0, f0)) - flags[1][:, None, None] * products(r1, f1)
        out = jnp.where(g.col == 0, p0, jnp.where(g.col == 1, p1, rest))
        return (out * listed[:, None, None])[:, None, None]

    return on_device


def solution(mesh):
    n_row = mesh.shape["row"]
    n_col = mesh.shape["col"]
    shape = (n_row // 2, 2, n_col // 4, 4)
    finer = Mesh(mesh.devices.reshape(shape), AXES)
    return jax.shard_map(
        make_on_device(shape),
        mesh=finer,
        in_specs=(P(None, ROW, COL, None, None), P(None, ROW, COL), P(None, None, ROW, COL)),
        out_specs=P(None, ROW, COL, None, None),
        check_vma=False,
    )
```

```python
import numpy as np
import jax
import jax.numpy as jnp
from jax import lax
from jax.sharding import Mesh
from jax.sharding import PartitionSpec as P

AXES = ("y", "core", "z", "x")
ROW = ("y", "core")
COL = ("z", "x")


def split_rounds(n, fan=2):
    spans = [(0, n)]
    rounds = []
    while any(length > 1 for _, length in spans):
        sends = [[] for _ in range(fan)]
        next_spans = []
        for start, length in spans:
            parts = min(fan + 1, length)
            sizes = [length // parts + (1 if i < length % parts else 0) for i in range(parts)]
            offset = start
            for i, size in enumerate(sizes):
                if i > 0:
                    sends[i - 1].append((start, offset))
                next_spans.append((offset, size))
                offset += size
        rounds.append([s for s in sends if s])
        spans = next_spans
    return rounds


class Grid:
    def __init__(self, shape):
        self.shape = shape
        ny, nk, nz, nx = shape
        self.n_row = ny * nk
        self.n_col = nz * nx
        self.y = lax.axis_index("y")
        self.core = lax.axis_index("core")
        self.z = lax.axis_index("z")
        self.x = lax.axis_index("x")
        self.row = self.y * nk + self.core
        self.col = self.z * nx + self.x
        self.lin = ((self.y * nk + self.core) * nz + self.z) * nx + self.x

    def index(self, y, k, z, x):
        ny, nk, nz, nx = self.shape
        return ((y * nk + k) * nz + z) * nx + x

    def send(self, value, pairs):
        perm = [(self.index(*s), self.index(*d)) for s, d in pairs]
        got = lax.ppermute(value, AXES, perm)
        mask = np.zeros(int(np.prod(self.shape)), bool)
        mask[[d for _, d in perm]] = True
        hit = jnp.asarray(mask)[self.lin]
        return got, hit

    def plan_down(self, roots):
        ny, nk, nz, nx = self.shape
        rounds = []
        pairs = []
        for c, r in roots.items():
            z, x = divmod(c, nx)
            y0, k0 = divmod(r, nk)
            for k in range(nk):
                if k != k0:
                    pairs.append(((y0, k0, z, x), (y0, k, z, x)))
        if pairs:
            rounds.append([pairs])
        for sends in split_rounds(ny):
            level = []
            for offsets in sends:
                pairs = []
                for c, r in roots.items():
                    z, x = divmod(c, nx)
                    y0 = r // nk
                    for a, b in offsets:
                        for k in range(nk):
                            pairs.append((((y0 + a) % ny, k, z, x), ((y0 + b) % ny, k, z, x)))
                level.append(pairs)
            rounds.append(level)
        return rounds

    def run(self, value, rounds):
        for level in rounds:
            results = [self.send(value, pairs) for pairs in level if pairs]
            for got, hit in results:
                value = jnp.where(hit, got, value)
        return value

    def down_columns(self, value, roots):
        return self.run(value, self.plan_down(roots))

    def along_rows(self, tiles, root_col, skip=()):
        ny, nk, nz, nx = self.shape
        slots = tiles.shape[0]
        assert slots == nx
        z0, x0 = divmod(root_col, nx)
        skipped = {divmod(c, nx) for c in skip}
        rows = [(y, k) for y in range(ny) for k in range(nk)]
        line_root = {x0: z0}
        held = tiles[0]
        for j in range(1, nx):
            x = (x0 + j) % nx
            z = z0
            while (z, x) in skipped:
                z = (z + 1) % nz
            line_root[x] = z
            pairs = [((y, k, z0, x0), (y, k, z, x)) for y, k in rows]
            got, hit = self.send(tiles[j], pairs)
            held = jnp.where(hit, got, held)
        trees = {}
        for x in range(nx):
            zs = [(line_root[x] + t) % nz for t in range(nz)]
            trees[x] = [z for z in zs if (z, x) not in skipped]
        depth = max(len(split_rounds(len(t))) for t in trees.values())
        plans = {x: split_rounds(len(t)) for x, t in trees.items()}
        for level in range(depth):
            fan = max(len(plans[x][level]) for x in plans if level < len(plans[x]))
            results = []
            for i in range(fan):
                pairs = []
                for x, plan in plans.items():
                    if level < len(plan) and i < len(plan[level]):
                        zs = trees[x]
                        for a, b in plan[level][i]:
                            pairs += [((y, k, zs[a], x), (y, k, zs[b], x)) for y, k in rows]
                if pairs:
                    results.append(self.send(held, pairs))
            for got, hit in results:
                held = jnp.where(hit, got, held)
        buffers = [held]
        table = np.zeros((int(np.prod(self.shape)), nx), np.int32)
        for d in range(1, nx):
            pairs = []
            for z in range(nz):
                for x in range(nx):
                    t = (x + d) % nx
                    if (z, x) in skipped or (z, t) in skipped or (z, t) == (z0, x0):
                        continue
                    pairs += [((y, k, z, x), (y, k, z, t)) for y, k in rows]
            if pairs:
                got, _ = self.send(held, pairs)
                buffers.append(got)
                for y, k in rows:
                    for z in range(nz):
                        for t in range(nx):
                            x = (t - d) % nx
                            if (z, x) not in skipped and (z, t) not in skipped:
                                table[self.index(y, k, z, t), (x - x0) % nx] = len(buffers) - 1
        for z, x in sorted(skipped):
            j = (x - x0) % nx
            for t in range(nx):
                if (z, t) in skipped or (z, t) == (z0, x0):
                    continue
                pairs = [((y, k, z0, x0), (y, k, z, t)) for y, k in rows]
                got, _ = self.send(tiles[j], pairs)
                buffers.append(got)
                for y, k in rows:
                    table[self.index(y, k, z, t), j] = len(buffers) - 1
        for y, k in rows:
            for z in range(nz):
                for x in range(nx):
                    table[self.index(y, k, z, x), (x - x0) % nx] = 0
        order = jnp.asarray(table)[self.lin]
        out = jnp.take(jnp.stack(buffers), order, axis=0)
        is_root = (self.z == z0) & (self.x == x0)
        return jnp.where(is_root, tiles, out)


def products(rows, far):
    return jnp.einsum("sab,db->sad", rows, far, precision=lax.Precision.HIGHEST)


def factor_and_inverse(tile):
    factor = jnp.linalg.cholesky(tile)
    eye = jnp.eye(tile.shape[-1], dtype=tile.dtype)
    return factor, jax.scipy.linalg.solve_triangular(factor, eye, lower=True)


def make_on_device(shape):
    def on_device(matrix, present, update):
        g = Grid(shape)
        ny, nk, nz, nx = shape
        tiles = matrix[:, 0, 0]
        listed = present[:, 0, 0].astype(jnp.float32)
        flags = update[:, :, 0, 0].astype(jnp.float32)
        width = tiles.shape[-1]
        n_row, n_col = g.n_row, g.n_col
        identity = jnp.eye(width, dtype=jnp.float32)
        far_slot = g.col // n_row
        far_root = {c: c % n_row for c in range(2, n_col)}
        rows = [(y, k) for y in range(ny) for k in range(nk)]
        owner0 = (g.row == 0) & (g.col == 0)
        owner1 = (g.row == 1) & (g.col == 1)

        a_row0, _ = g.send(tiles, [((y, k, 0, 0), (y, k, 0, 1)) for y, k in rows])
        a10, _ = g.send(tiles[0], [((0, 1, 0, 0), (0, 1, 0, 1))])
        a10 = g.down_columns(a10, {1: 1})

        factor0, inverse0 = lax.cond(owner0, factor_and_inverse, lambda t: (identity, identity), tiles[0])
        first = g.plan_down({0: 0})
        second = g.plan_down({1: 0})
        joint = [first[0] + [[((0, 0, 0, 0), (0, 0, 0, 1))]]]
        for level in range(1, max(len(first), len(second) + 1)):
            here = first[level] if level < len(first) else []
            there = second[level - 1] if level - 1 < len(second) else []
            merged = [a + b for a, b in zip(here, there)] + here[len(there):] + there[len(here):]
            joint.append(merged)
        inverse0 = g.run(inverse0, joint)
        source0 = jnp.where(g.col == 1, a_row0, tiles)
        p0 = lax.cond((g.col == 0) | (g.col == 1), lambda d: products(d, inverse0), lambda d: d, source0)
        far01 = products(a10[None], inverse0)[0]
        work1 = tiles - flags[0][:, None, None] * products(p0, far01)
        factor1, inverse1 = lax.cond(owner1, factor_and_inverse, lambda t: (identity, identity), work1[0])
        inverse1 = g.down_columns(inverse1, {1: 1})
        p1 = lax.cond(g.col == 1, lambda d: products(d, inverse1), lambda d: d, work1)
        p1 = p1.at[0].set(jnp.where(owner1, factor1, p1[0]))
        p0 = p0.at[0].set(jnp.where(owner0, factor0, p0[0]))

        r0 = g.along_rows(p0, 0, skip=(1,))
        f0 = g.down_columns(lax.dynamic_index_in_dim(r0, far_slot, 0, keepdims=False), far_root)
        r1 = g.along_rows(p1, 1, skip=(0,))
        f1 = g.down_columns(lax.dynamic_index_in_dim(r1, far_slot, 0, keepdims=False), far_root)
        rest = (tiles - flags[0][:, None, None] * products(r0, f0)) - flags[1][:, None, None] * products(r1, f1)
        out = jnp.where(g.col == 0, p0, jnp.where(g.col == 1, p1, rest))
        return (out * listed[:, None, None])[:, None, None]

    return on_device


def solution(mesh):
    n_row = mesh.shape["row"]
    n_col = mesh.shape["col"]
    shape = (n_row // 2, 2, n_col // 4, 4)
    finer = Mesh(mesh.devices.reshape(shape), AXES)
    return jax.shard_map(
        make_on_device(shape),
        mesh=finer,
        in_specs=(P(None, ROW, COL, None, None), P(None, ROW, COL), P(None, None, ROW, COL)),
        out_specs=P(None, ROW, COL, None, None),
        check_vma=False,
    )
```

```python
import numpy as np
import jax
import jax.numpy as jnp
from jax import lax
from jax.sharding import Mesh
from jax.sharding import PartitionSpec as P

AXES = ("y", "core", "z", "x")
ROW = ("y", "core")
COL = ("z", "x")


def split_rounds(n, fan=2):
    spans = [(0, n)]
    rounds = []
    while any(length > 1 for _, length in spans):
        sends = [[] for _ in range(fan)]
        next_spans = []
        for start, length in spans:
            parts = min(fan + 1, length)
            sizes = [length // parts + (1 if i < length % parts else 0) for i in range(parts)]
            offset = start
            for i, size in enumerate(sizes):
                if i > 0:
                    sends[i - 1].append((start, offset))
                next_spans.append((offset, size))
                offset += size
        rounds.append([s for s in sends if s])
        spans = next_spans
    return rounds


class Grid:
    def __init__(self, shape):
        self.shape = shape
        ny, nk, nz, nx = shape
        self.n_row = ny * nk
        self.n_col = nz * nx
        self.y = lax.axis_index("y")
        self.core = lax.axis_index("core")
        self.z = lax.axis_index("z")
        self.x = lax.axis_index("x")
        self.row = self.y * nk + self.core
        self.col = self.z * nx + self.x
        self.lin = ((self.y * nk + self.core) * nz + self.z) * nx + self.x

    def index(self, y, k, z, x):
        ny, nk, nz, nx = self.shape
        return ((y * nk + k) * nz + z) * nx + x

    def send(self, value, pairs):
        perm = [(self.index(*s), self.index(*d)) for s, d in pairs]
        got = lax.ppermute(value, AXES, perm)
        mask = np.zeros(int(np.prod(self.shape)), bool)
        mask[[d for _, d in perm]] = True
        hit = jnp.asarray(mask)[self.lin]
        return got, hit

    def down_columns(self, value, roots):
        ny, nk, nz, nx = self.shape
        pairs = []
        for c, r in roots.items():
            z, x = divmod(c, nx)
            y0, k0 = divmod(r, nk)
            for k in range(nk):
                if k != k0:
                    pairs.append(((y0, k0, z, x), (y0, k, z, x)))
        if pairs:
            got, hit = self.send(value, pairs)
            value = jnp.where(hit, got, value)
        for sends in split_rounds(ny):
            results = []
            for offsets in sends:
                pairs = []
                for c, r in roots.items():
                    z, x = divmod(c, nx)
                    y0 = r // nk
                    for a, b in offsets:
                        for k in range(nk):
                            pairs.append((((y0 + a) % ny, k, z, x), ((y0 + b) % ny, k, z, x)))
                results.append(self.send(value, pairs))
            for got, hit in results:
                value = jnp.where(hit, got, value)
        return value

    def along_rows(self, tiles, root_col):
        ny, nk, nz, nx = self.shape
        slots = tiles.shape[0]
        z0, x0 = divmod(root_col, nx)
        rows = [(y, k) for y in range(ny) for k in range(nk)]
        assert slots == nx
        held = tiles[0]
        for j in range(1, nx):
            pairs = [((y, k, z0, x0), (y, k, z0, (x0 + j) % nx)) for y, k in rows]
            got, hit = self.send(tiles[j], pairs)
            held = jnp.where(hit, got, held)
        for sends in split_rounds(nz):
            results = []
            for offsets in sends:
                pairs = [
                    ((y, k, (z0 + a) % nz, x), (y, k, (z0 + b) % nz, x))
                    for y, k in rows
                    for x in range(nx)
                    for a, b in offsets
                ]
                results.append(self.send(held, pairs))
            for got, hit in results:
                held = jnp.where(hit, got, held)
        pieces = {0: held}
        left = held
        right = held
        for step in range(1, (nx - 1) // 2 + 2):
            if len(pieces) >= nx:
                break
            shift = [((y, k, z, x), (y, k, z, (x + 1) % nx)) for y, k in rows for z in range(nz) for x in range(nx)]
            left, _ = self.send(left, shift)
            pieces[-step] = left
            if len(pieces) >= nx:
                break
            shift = [((y, k, z, x), (y, k, z, (x - 1) % nx)) for y, k in rows for z in range(nz) for x in range(nx)]
            right, _ = self.send(right, shift)
            pieces[step] = right
        offsets = sorted(pieces)
        stack = jnp.stack([pieces[o] for o in offsets])
        base = (self.x - x0) % nx
        order = []
        for j in range(nx):
            pick = jnp.zeros((), jnp.int32)
            for i, o in enumerate(offsets):
                pick = jnp.where((base + o) % nx == j, i, pick)
            order.append(pick)
        return jnp.take(stack, jnp.stack(order), axis=0)


def solve_panel(factor, blocks):
    count = blocks.shape[0]
    width = blocks.shape[-1]
    stacked = jnp.transpose(blocks, (2, 0, 1)).reshape(width, count * width)
    solved = jax.scipy.linalg.solve_triangular(factor, stacked, lower=True)
    return jnp.transpose(solved.reshape(width, count, width), (1, 2, 0))


def products(rows, far):
    return jnp.einsum("sab,db->sad", rows, far, precision=lax.Precision.HIGHEST)


def make_on_device(shape):
    def on_device(matrix, present, update):
        g = Grid(shape)
        tiles = matrix[:, 0, 0]
        listed = present[:, 0, 0].astype(jnp.float32)
        flags = update[:, :, 0, 0].astype(jnp.float32)
        width = tiles.shape[-1]
        slots = tiles.shape[0]
        n_row, n_col = g.n_row, g.n_col
        identity = jnp.eye(width, dtype=jnp.float32)
        far_slot = g.col // n_row
        far_root = {c: c % n_row for c in range(2, n_col)}

        def panel_factor(work, k):
            owner = (g.row == k) & (g.col == k)
            factor = jnp.linalg.cholesky(jnp.where(owner, work[0], identity))
            factor = g.down_columns(factor, {k: k})
            solved = lax.cond(g.col == k, lambda d: solve_panel(factor, d), lambda d: d, work)
            return solved.at[0].set(jnp.where(owner, factor, solved[0]))

        p0 = panel_factor(tiles, 0)
        pairs = [((y, k, 0, 0), (y, k, 0, 1)) for y in range(shape[0]) for k in range(shape[1])]
        r01, _ = g.send(p0, pairs)
        f01 = g.down_columns(r01[1 // n_row], {1: 1 % n_row})
        work1 = tiles - flags[0][:, None, None] * products(r01, f01)
        p1 = panel_factor(work1, 1)

        both = jnp.stack([r01, p1], axis=1)
        rows_both = g.along_rows(both, 1)
        far = g.down_columns(lax.dynamic_index_in_dim(rows_both, far_slot, 0, keepdims=False), far_root)
        rest = (tiles - flags[0][:, None, None] * products(rows_both[:, 0], far[0])) - flags[1][
            :, None, None
        ] * products(rows_both[:, 1], far[1])
        out = jnp.where(g.col == 0, p0, jnp.where(g.col == 1, p1, rest))
        return (out * listed[:, None, None])[:, None, None]

    return on_device


def solution(mesh):
    n_row = mesh.shape["row"]
    n_col = mesh.shape["col"]
    shape = (n_row // 2, 2, n_col // 4, 4)
    finer = Mesh(mesh.devices.reshape(shape), AXES)
    return jax.shard_map(
        make_on_device(shape),
        mesh=finer,
        in_specs=(P(None, ROW, COL, None, None), P(None, ROW, COL), P(None, None, ROW, COL)),
        out_specs=P(None, ROW, COL, None, None),
        check_vma=False,
    )
```

```python
import numpy as np
import jax
import jax.numpy as jnp
from jax import lax
from jax.sharding import Mesh
from jax.sharding import PartitionSpec as P

AXES = ("y", "core", "z", "x")
ROW = ("y", "core")
COL = ("z", "x")


def split_rounds(n, fan=1):
    spans = [(0, n)]
    rounds = []
    while any(length > 1 for _, length in spans):
        sends = [[] for _ in range(fan)]
        next_spans = []
        for start, length in spans:
            parts = min(fan + 1, length)
            sizes = [length // parts + (1 if i < length % parts else 0) for i in range(parts)]
            offset = start
            for i, size in enumerate(sizes):
                if i > 0:
                    sends[i - 1].append((start, offset))
                next_spans.append((offset, size))
                offset += size
        rounds.append([s for s in sends if s])
        spans = next_spans
    return rounds


class Grid:
    def __init__(self, shape):
        self.shape = shape
        ny, nk, nz, nx = shape
        self.n_row = ny * nk
        self.n_col = nz * nx
        self.y = lax.axis_index("y")
        self.core = lax.axis_index("core")
        self.z = lax.axis_index("z")
        self.x = lax.axis_index("x")
        self.row = self.y * nk + self.core
        self.col = self.z * nx + self.x
        self.lin = ((self.y * nk + self.core) * nz + self.z) * nx + self.x

    def index(self, y, k, z, x):
        ny, nk, nz, nx = self.shape
        return ((y * nk + k) * nz + z) * nx + x

    def send(self, value, pairs):
        perm = [(self.index(*s), self.index(*d)) for s, d in pairs]
        got = lax.ppermute(value, AXES, perm)
        mask = np.zeros(int(np.prod(self.shape)), bool)
        mask[[d for _, d in perm]] = True
        hit = jnp.asarray(mask)[self.lin]
        return got, hit

    def down_columns(self, value, roots):
        ny, nk, nz, nx = self.shape
        pairs = []
        for c, r in roots.items():
            z, x = divmod(c, nx)
            y0, k0 = divmod(r, nk)
            for k in range(nk):
                if k != k0:
                    pairs.append(((y0, k0, z, x), (y0, k, z, x)))
        if pairs:
            got, hit = self.send(value, pairs)
            value = jnp.where(hit, got, value)
        for sends in split_rounds(ny):
            results = []
            for offsets in sends:
                pairs = []
                for c, r in roots.items():
                    z, x = divmod(c, nx)
                    y0 = r // nk
                    for a, b in offsets:
                        for k in range(nk):
                            pairs.append((((y0 + a) % ny, k, z, x), ((y0 + b) % ny, k, z, x)))
                results.append(self.send(value, pairs))
            for got, hit in results:
                value = jnp.where(hit, got, value)
        return value

    def along_rows(self, tiles, root_col):
        ny, nk, nz, nx = self.shape
        slots = tiles.shape[0]
        z0, x0 = divmod(root_col, nx)
        rows = [(y, k) for y in range(ny) for k in range(nk)]
        assert slots == nx
        held = tiles[0]
        for j in range(1, nx):
            pairs = [((y, k, z0, x0), (y, k, z0, (x0 + j) % nx)) for y, k in rows]
            got, hit = self.send(tiles[j], pairs)
            held = jnp.where(hit, got, held)
        for sends in split_rounds(nz):
            results = []
            for offsets in sends:
                pairs = [
                    ((y, k, (z0 + a) % nz, x), (y, k, (z0 + b) % nz, x))
                    for y, k in rows
                    for x in range(nx)
                    for a, b in offsets
                ]
                results.append(self.send(held, pairs))
            for got, hit in results:
                held = jnp.where(hit, got, held)
        pieces = {0: held}
        left = held
        right = held
        for step in range(1, (nx - 1) // 2 + 2):
            if len(pieces) >= nx:
                break
            shift = [((y, k, z, x), (y, k, z, (x + 1) % nx)) for y, k in rows for z in range(nz) for x in range(nx)]
            left, _ = self.send(left, shift)
            pieces[-step] = left
            if len(pieces) >= nx:
                break
            shift = [((y, k, z, x), (y, k, z, (x - 1) % nx)) for y, k in rows for z in range(nz) for x in range(nx)]
            right, _ = self.send(right, shift)
            pieces[step] = right
        offsets = sorted(pieces)
        stack = jnp.stack([pieces[o] for o in offsets])
        base = (self.x - x0) % nx
        order = []
        for j in range(nx):
            pick = jnp.zeros((), jnp.int32)
            for i, o in enumerate(offsets):
                pick = jnp.where((base + o) % nx == j, i, pick)
            order.append(pick)
        return jnp.take(stack, jnp.stack(order), axis=0)


def solve_panel(factor, blocks):
    count = blocks.shape[0]
    width = blocks.shape[-1]
    stacked = jnp.transpose(blocks, (2, 0, 1)).reshape(width, count * width)
    solved = jax.scipy.linalg.solve_triangular(factor, stacked, lower=True)
    return jnp.transpose(solved.reshape(width, count, width), (1, 2, 0))


def products(rows, far):
    return jnp.einsum("sab,db->sad", rows, far, precision=lax.Precision.HIGHEST)


def make_on_device(shape):
    def on_device(matrix, present, update):
        g = Grid(shape)
        tiles = matrix[:, 0, 0]
        listed = present[:, 0, 0].astype(jnp.float32)
        flags = update[:, :, 0, 0].astype(jnp.float32)
        width = tiles.shape[-1]
        slots = tiles.shape[0]
        n_row, n_col = g.n_row, g.n_col
        identity = jnp.eye(width, dtype=jnp.float32)
        far_slot = g.col // n_row
        far_root = {c: c % n_row for c in range(2, n_col)}

        def panel_factor(work, k):
            owner = (g.row == k) & (g.col == k)
            factor = jnp.linalg.cholesky(jnp.where(owner, work[0], identity))
            factor = g.down_columns(factor, {k: k})
            solved = lax.cond(g.col == k, lambda d: solve_panel(factor, d), lambda d: d, work)
            return solved.at[0].set(jnp.where(owner, factor, solved[0]))

        p0 = panel_factor(tiles, 0)
        pairs = [((y, k, 0, 0), (y, k, 0, 1)) for y in range(shape[0]) for k in range(shape[1])]
        r01, _ = g.send(p0, pairs)
        head = r01[1 // n_row]
        work11 = tiles[0] - flags[0, 0] * products(head[None], head)[0]
        owner1 = (g.row == 1) & (g.col == 1)
        factor1 = jnp.linalg.cholesky(jnp.where(owner1, work11, identity))
        sent = g.down_columns(jnp.stack([factor1, head]), {1: 1 % n_row})
        work1 = tiles - flags[0][:, None, None] * products(r01, sent[1])
        p1 = lax.cond(g.col == 1, lambda d: solve_panel(sent[0], d), lambda d: d, work1)
        p1 = p1.at[0].set(jnp.where(owner1, factor1, p1[0]))

        both = jnp.stack([r01, p1], axis=1)
        rows_both = g.along_rows(both, 1)
        far = g.down_columns(lax.dynamic_index_in_dim(rows_both, far_slot, 0, keepdims=False), far_root)
        rest = (tiles - flags[0][:, None, None] * products(rows_both[:, 0], far[0])) - flags[1][
            :, None, None
        ] * products(rows_both[:, 1], far[1])
        out = jnp.where(g.col == 0, p0, jnp.where(g.col == 1, p1, rest))
        return (out * listed[:, None, None])[:, None, None]

    return on_device


def solution(mesh):
    n_row = mesh.shape["row"]
    n_col = mesh.shape["col"]
    shape = (n_row // 2, 2, n_col // 4, 4)
    finer = Mesh(mesh.devices.reshape(shape), AXES)
    return jax.shard_map(
        make_on_device(shape),
        mesh=finer,
        in_specs=(P(None, ROW, COL, None, None), P(None, ROW, COL), P(None, None, ROW, COL)),
        out_specs=P(None, ROW, COL, None, None),
        check_vma=False,
    )
```

```python
import numpy as np
import jax
import jax.numpy as jnp
from jax import lax
from jax.sharding import Mesh
from jax.sharding import PartitionSpec as P

AXES = ("y", "core", "z", "x")
ROW = ("y", "core")
COL = ("z", "x")


def split_rounds(n, fan=1):
    spans = [(0, n)]
    rounds = []
    while any(length > 1 for _, length in spans):
        sends = [[] for _ in range(fan)]
        next_spans = []
        for start, length in spans:
            parts = min(fan + 1, length)
            sizes = [length // parts + (1 if i < length % parts else 0) for i in range(parts)]
            offset = start
            for i, size in enumerate(sizes):
                if i > 0:
                    sends[i - 1].append((start, offset))
                next_spans.append((offset, size))
                offset += size
        rounds.append([s for s in sends if s])
        spans = next_spans
    return rounds


class Grid:
    def __init__(self, shape):
        self.shape = shape
        ny, nk, nz, nx = shape
        self.n_row = ny * nk
        self.n_col = nz * nx
        self.y = lax.axis_index("y")
        self.core = lax.axis_index("core")
        self.z = lax.axis_index("z")
        self.x = lax.axis_index("x")
        self.row = self.y * nk + self.core
        self.col = self.z * nx + self.x
        self.lin = ((self.y * nk + self.core) * nz + self.z) * nx + self.x

    def index(self, y, k, z, x):
        ny, nk, nz, nx = self.shape
        return ((y * nk + k) * nz + z) * nx + x

    def send(self, value, pairs):
        perm = [(self.index(*s), self.index(*d)) for s, d in pairs]
        got = lax.ppermute(value, AXES, perm)
        mask = np.zeros(int(np.prod(self.shape)), bool)
        mask[[d for _, d in perm]] = True
        hit = jnp.asarray(mask)[self.lin]
        return got, hit

    def down_columns(self, value, roots):
        ny, nk, nz, nx = self.shape
        pairs = []
        for c, r in roots.items():
            z, x = divmod(c, nx)
            y0, k0 = divmod(r, nk)
            for k in range(nk):
                if k != k0:
                    pairs.append(((y0, k0, z, x), (y0, k, z, x)))
        if pairs:
            got, hit = self.send(value, pairs)
            value = jnp.where(hit, got, value)
        for sends in split_rounds(ny):
            results = []
            for offsets in sends:
                pairs = []
                for c, r in roots.items():
                    z, x = divmod(c, nx)
                    y0 = r // nk
                    for a, b in offsets:
                        for k in range(nk):
                            pairs.append((((y0 + a) % ny, k, z, x), ((y0 + b) % ny, k, z, x)))
                results.append(self.send(value, pairs))
            for got, hit in results:
                value = jnp.where(hit, got, value)
        return value

    def along_rows(self, tiles, root_col):
        ny, nk, nz, nx = self.shape
        slots = tiles.shape[0]
        z0, x0 = divmod(root_col, nx)
        rows = [(y, k) for y in range(ny) for k in range(nk)]
        assert slots == nx
        held = tiles[0]
        for j in range(1, nx):
            pairs = [((y, k, z0, x0), (y, k, z0, (x0 + j) % nx)) for y, k in rows]
            got, hit = self.send(tiles[j], pairs)
            held = jnp.where(hit, got, held)
        for sends in split_rounds(nz):
            results = []
            for offsets in sends:
                pairs = [
                    ((y, k, (z0 + a) % nz, x), (y, k, (z0 + b) % nz, x))
                    for y, k in rows
                    for x in range(nx)
                    for a, b in offsets
                ]
                results.append(self.send(held, pairs))
            for got, hit in results:
                held = jnp.where(hit, got, held)
        pieces = {0: held}
        left = held
        right = held
        for step in range(1, (nx - 1) // 2 + 2):
            if len(pieces) >= nx:
                break
            shift = [((y, k, z, x), (y, k, z, (x + 1) % nx)) for y, k in rows for z in range(nz) for x in range(nx)]
            left, _ = self.send(left, shift)
            pieces[-step] = left
            if len(pieces) >= nx:
                break
            shift = [((y, k, z, x), (y, k, z, (x - 1) % nx)) for y, k in rows for z in range(nz) for x in range(nx)]
            right, _ = self.send(right, shift)
            pieces[step] = right
        offsets = sorted(pieces)
        stack = jnp.stack([pieces[o] for o in offsets])
        base = (self.x - x0) % nx
        order = []
        for j in range(nx):
            pick = jnp.zeros((), jnp.int32)
            for i, o in enumerate(offsets):
                pick = jnp.where((base + o) % nx == j, i, pick)
            order.append(pick)
        return jnp.take(stack, jnp.stack(order), axis=0)


def solve_panel(factor, blocks):
    count = blocks.shape[0]
    width = blocks.shape[-1]
    stacked = jnp.transpose(blocks, (2, 0, 1)).reshape(width, count * width)
    solved = jax.scipy.linalg.solve_triangular(factor, stacked, lower=True)
    return jnp.transpose(solved.reshape(width, count, width), (1, 2, 0))


def products(rows, far):
    return jnp.einsum("sab,db->sad", rows, far, precision=lax.Precision.HIGHEST)


def make_on_device(shape):
    def on_device(matrix, present, update):
        g = Grid(shape)
        tiles = matrix[:, 0, 0]
        listed = present[:, 0, 0].astype(jnp.float32)
        flags = update[:, :, 0, 0].astype(jnp.float32)
        width = tiles.shape[-1]
        slots = tiles.shape[0]
        n_row, n_col = g.n_row, g.n_col
        identity = jnp.eye(width, dtype=jnp.float32)
        far_slot = g.col // n_row
        far_root = {c: c % n_row for c in range(2, n_col)}

        rows = [(y, k) for y in range(shape[0]) for k in range(shape[1])]
        a_row0, _ = g.send(tiles, [((y, k, 0, 0), (y, k, 0, 1)) for y, k in rows])
        a00, _ = g.send(tiles[0], [((0, 0, 0, 0), (0, 0, 0, 1))])
        a00 = g.down_columns(a00, {1: 0})

        owner0 = (g.row == 0) & (g.col == 0)
        second = g.col == 1
        diag0 = jnp.where(second, a00, tiles[0])
        factor0 = jnp.linalg.cholesky(jnp.where(owner0 | second, diag0, identity))
        spread0 = g.down_columns(factor0, {0: 0})
        factor0 = jnp.where(second, factor0, spread0)
        source0 = jnp.where(second, a_row0, tiles)
        p0 = lax.cond((g.col == 0) | second, lambda d: solve_panel(factor0, d), lambda d: d, source0)
        p0 = p0.at[0].set(jnp.where(owner0, factor0, p0[0]))

        head = p0[1 // n_row]
        work11 = tiles[0] - flags[0, 0] * products(head[None], head)[0]
        owner1 = (g.row == 1) & second
        factor1 = jnp.linalg.cholesky(jnp.where(owner1, work11, identity))
        sent = g.down_columns(jnp.stack([factor1, head]), {1: 1 % n_row})
        work1 = tiles - flags[0][:, None, None] * products(p0, sent[1])
        p1 = lax.cond(second, lambda d: solve_panel(sent[0], d), lambda d: d, work1)
        p1 = p1.at[0].set(jnp.where(owner1, factor1, p1[0]))
        r01 = p0

        both = jnp.stack([r01, p1], axis=1)
        rows_both = g.along_rows(both, 1)
        far = g.down_columns(lax.dynamic_index_in_dim(rows_both, far_slot, 0, keepdims=False), far_root)
        rest = (tiles - flags[0][:, None, None] * products(rows_both[:, 0], far[0])) - flags[1][
            :, None, None
        ] * products(rows_both[:, 1], far[1])
        out = jnp.where(g.col == 0, p0, jnp.where(g.col == 1, p1, rest))
        return (out * listed[:, None, None])[:, None, None]

    return on_device


def solution(mesh):
    n_row = mesh.shape["row"]
    n_col = mesh.shape["col"]
    shape = (n_row // 2, 2, n_col // 4, 4)
    finer = Mesh(mesh.devices.reshape(shape), AXES)
    return jax.shard_map(
        make_on_device(shape),
        mesh=finer,
        in_specs=(P(None, ROW, COL, None, None), P(None, ROW, COL), P(None, None, ROW, COL)),
        out_specs=P(None, ROW, COL, None, None),
        check_vma=False,
    )
```

```python
import numpy as np
import jax
import jax.numpy as jnp
from jax import lax
from jax.sharding import Mesh
from jax.sharding import PartitionSpec as P

AXES = ("y", "core", "z", "x")
ROW = ("y", "core")
COL = ("z", "x")


def split_rounds(n, fan=1):
    spans = [(0, n)]
    rounds = []
    while any(length > 1 for _, length in spans):
        sends = [[] for _ in range(fan)]
        next_spans = []
        for start, length in spans:
            parts = min(fan + 1, length)
            sizes = [length // parts + (1 if i < length % parts else 0) for i in range(parts)]
            offset = start
            for i, size in enumerate(sizes):
                if i > 0:
                    sends[i - 1].append((start, offset))
                next_spans.append((offset, size))
                offset += size
        rounds.append([s for s in sends if s])
        spans = next_spans
    return rounds


class Grid:
    def __init__(self, shape):
        self.shape = shape
        ny, nk, nz, nx = shape
        self.n_row = ny * nk
        self.n_col = nz * nx
        self.y = lax.axis_index("y")
        self.core = lax.axis_index("core")
        self.z = lax.axis_index("z")
        self.x = lax.axis_index("x")
        self.row = self.y * nk + self.core
        self.col = self.z * nx + self.x
        self.lin = ((self.y * nk + self.core) * nz + self.z) * nx + self.x

    def index(self, y, k, z, x):
        ny, nk, nz, nx = self.shape
        return ((y * nk + k) * nz + z) * nx + x

    def send(self, value, pairs):
        perm = [(self.index(*s), self.index(*d)) for s, d in pairs]
        got = lax.ppermute(value, AXES, perm)
        mask = np.zeros(int(np.prod(self.shape)), bool)
        mask[[d for _, d in perm]] = True
        hit = jnp.asarray(mask)[self.lin]
        return got, hit

    def down_columns(self, value, roots):
        ny, nk, nz, nx = self.shape
        pairs = []
        for c, r in roots.items():
            z, x = divmod(c, nx)
            y0, k0 = divmod(r, nk)
            for k in range(nk):
                if k != k0:
                    pairs.append(((y0, k0, z, x), (y0, k, z, x)))
        if pairs:
            got, hit = self.send(value, pairs)
            value = jnp.where(hit, got, value)
        for sends in split_rounds(ny):
            results = []
            for offsets in sends:
                pairs = []
                for c, r in roots.items():
                    z, x = divmod(c, nx)
                    y0 = r // nk
                    for a, b in offsets:
                        for k in range(nk):
                            pairs.append((((y0 + a) % ny, k, z, x), ((y0 + b) % ny, k, z, x)))
                results.append(self.send(value, pairs))
            for got, hit in results:
                value = jnp.where(hit, got, value)
        return value

    def along_rows(self, tiles, root_col):
        ny, nk, nz, nx = self.shape
        slots = tiles.shape[0]
        z0, x0 = divmod(root_col, nx)
        rows = [(y, k) for y in range(ny) for k in range(nk)]
        assert slots == nx
        held = tiles[0]
        for j in range(1, nx):
            pairs = [((y, k, z0, x0), (y, k, z0, (x0 + j) % nx)) for y, k in rows]
            got, hit = self.send(tiles[j], pairs)
            held = jnp.where(hit, got, held)
        for sends in split_rounds(nz):
            results = []
            for offsets in sends:
                pairs = [
                    ((y, k, (z0 + a) % nz, x), (y, k, (z0 + b) % nz, x))
                    for y, k in rows
                    for x in range(nx)
                    for a, b in offsets
                ]
                results.append(self.send(held, pairs))
            for got, hit in results:
                held = jnp.where(hit, got, held)
        pieces = {0: held}
        left = held
        right = held
        for step in range(1, (nx - 1) // 2 + 2):
            if len(pieces) >= nx:
                break
            shift = [((y, k, z, x), (y, k, z, (x + 1) % nx)) for y, k in rows for z in range(nz) for x in range(nx)]
            left, _ = self.send(left, shift)
            pieces[-step] = left
            if len(pieces) >= nx:
                break
            shift = [((y, k, z, x), (y, k, z, (x - 1) % nx)) for y, k in rows for z in range(nz) for x in range(nx)]
            right, _ = self.send(right, shift)
            pieces[step] = right
        offsets = sorted(pieces)
        stack = jnp.stack([pieces[o] for o in offsets])
        base = (self.x - x0) % nx
        order = []
        for j in range(nx):
            pick = jnp.zeros((), jnp.int32)
            for i, o in enumerate(offsets):
                pick = jnp.where((base + o) % nx == j, i, pick)
            order.append(pick)
        return jnp.take(stack, jnp.stack(order), axis=0)


def solve_panel(factor, blocks):
    count = blocks.shape[0]
    width = blocks.shape[-1]
    stacked = jnp.transpose(blocks, (2, 0, 1)).reshape(width, count * width)
    solved = jax.scipy.linalg.solve_triangular(factor, stacked, lower=True)
    return jnp.transpose(solved.reshape(width, count, width), (1, 2, 0))


def products(rows, far):
    return jnp.einsum("sab,db->sad", rows, far, precision=lax.Precision.HIGHEST)


def make_on_device(shape):
    def on_device(matrix, present, update):
        g = Grid(shape)
        tiles = matrix[:, 0, 0]
        listed = present[:, 0, 0].astype(jnp.float32)
        flags = update[:, :, 0, 0].astype(jnp.float32)
        width = tiles.shape[-1]
        slots = tiles.shape[0]
        n_row, n_col = g.n_row, g.n_col
        identity = jnp.eye(width, dtype=jnp.float32)
        far_slot = g.col // n_row
        far_root = {c: c % n_row for c in range(2, n_col)}

        rows = [(y, k) for y in range(shape[0]) for k in range(shape[1])]
        ny, nk = shape[0], shape[1]
        first, second = g.col == 0, g.col == 1
        a_row0, _ = g.send(tiles, [((y, k, 0, 0), (y, k, 0, 1)) for y, k in rows])
        got, hit = g.send(tiles[0], [((0, 0, 0, 0), (0, 0, 0, 1)), ((0, 1, 0, 0), (0, 1, 0, 1))])
        mine = jnp.where(hit, got, tiles[0])
        other, _ = g.send(mine, [((0, a, 0, c), (0, 1 - a, 0, c)) for a in range(2) for c in range(2)])
        pair = jnp.where(g.core == 0, jnp.stack([mine, other]), jnp.stack([other, mine]))
        for sends in split_rounds(ny):
            for offsets in sends:
                pairs = [((a, k, 0, c), (b, k, 0, c)) for a, b in offsets for k in range(nk) for c in range(2)]
                got, hit = g.send(pair, pairs)
                pair = jnp.where(hit, got, pair)
        a00, a10 = pair[0], pair[1]

        owner0 = (g.row == 0) & first
        factor0 = jnp.linalg.cholesky(jnp.where(first | second, a00, identity))
        source0 = jnp.concatenate([jnp.where(second, a_row0, tiles), a10[None]])
        solved0 = lax.cond(first | second, lambda d: solve_panel(factor0, d), lambda d: d, source0)
        p0 = solved0[:slots]
        p0 = p0.at[0].set(jnp.where(owner0, factor0, p0[0]))
        head = solved0[slots]

        work1 = tiles - flags[0][:, None, None] * products(p0, head)
        owner1 = (g.row == 1) & second
        factor1 = jnp.linalg.cholesky(jnp.where(owner1, work1[0], identity))
        spread1 = g.down_columns(factor1, {1: 1 % n_row})
        p1 = lax.cond(second, lambda d: solve_panel(spread1, d), lambda d: d, work1)
        p1 = p1.at[0].set(jnp.where(owner1, factor1, p1[0]))
        r01 = p0

        both = jnp.stack([r01, p1], axis=1)
        rows_both = g.along_rows(both, 1)
        far = g.down_columns(lax.dynamic_index_in_dim(rows_both, far_slot, 0, keepdims=False), far_root)
        rest = (tiles - flags[0][:, None, None] * products(rows_both[:, 0], far[0])) - flags[1][
            :, None, None
        ] * products(rows_both[:, 1], far[1])
        out = jnp.where(g.col == 0, p0, jnp.where(g.col == 1, p1, rest))
        return (out * listed[:, None, None])[:, None, None]

    return on_device


def solution(mesh):
    n_row = mesh.shape["row"]
    n_col = mesh.shape["col"]
    shape = (n_row // 2, 2, n_col // 4, 4)
    finer = Mesh(mesh.devices.reshape(shape), AXES)
    return jax.shard_map(
        make_on_device(shape),
        mesh=finer,
        in_specs=(P(None, ROW, COL, None, None), P(None, ROW, COL), P(None, None, ROW, COL)),
        out_specs=P(None, ROW, COL, None, None),
        check_vma=False,
    )
```

```python
import numpy as np
import jax
import jax.numpy as jnp
from jax import lax
from jax.sharding import Mesh
from jax.sharding import PartitionSpec as P

AXES = ("y", "core", "z", "x")
ROW = ("y", "core")
COL = ("z", "x")


def split_rounds(n, fan=1):
    spans = [(0, n)]
    rounds = []
    while any(length > 1 for _, length in spans):
        sends = [[] for _ in range(fan)]
        next_spans = []
        for start, length in spans:
            parts = min(fan + 1, length)
            sizes = [length // parts + (1 if i < length % parts else 0) for i in range(parts)]
            offset = start
            for i, size in enumerate(sizes):
                if i > 0:
                    sends[i - 1].append((start, offset))
                next_spans.append((offset, size))
                offset += size
        rounds.append([s for s in sends if s])
        spans = next_spans
    return rounds


class Grid:
    def __init__(self, shape):
        self.shape = shape
        ny, nk, nz, nx = shape
        self.n_row = ny * nk
        self.n_col = nz * nx
        self.y = lax.axis_index("y")
        self.core = lax.axis_index("core")
        self.z = lax.axis_index("z")
        self.x = lax.axis_index("x")
        self.row = self.y * nk + self.core
        self.col = self.z * nx + self.x
        self.lin = ((self.y * nk + self.core) * nz + self.z) * nx + self.x

    def index(self, y, k, z, x):
        ny, nk, nz, nx = self.shape
        return ((y * nk + k) * nz + z) * nx + x

    def send(self, value, pairs):
        perm = [(self.index(*s), self.index(*d)) for s, d in pairs]
        got = lax.ppermute(value, AXES, perm)
        mask = np.zeros(int(np.prod(self.shape)), bool)
        mask[[d for _, d in perm]] = True
        hit = jnp.asarray(mask)[self.lin]
        return got, hit

    def down_columns(self, value, roots):
        ny, nk, nz, nx = self.shape
        pairs = []
        for c, r in roots.items():
            z, x = divmod(c, nx)
            y0, k0 = divmod(r, nk)
            for k in range(nk):
                if k != k0:
                    pairs.append(((y0, k0, z, x), (y0, k, z, x)))
        if pairs:
            got, hit = self.send(value, pairs)
            value = jnp.where(hit, got, value)
        for sends in split_rounds(ny):
            results = []
            for offsets in sends:
                pairs = []
                for c, r in roots.items():
                    z, x = divmod(c, nx)
                    y0 = r // nk
                    for a, b in offsets:
                        for k in range(nk):
                            pairs.append((((y0 + a) % ny, k, z, x), ((y0 + b) % ny, k, z, x)))
                results.append(self.send(value, pairs))
            for got, hit in results:
                value = jnp.where(hit, got, value)
        return value

    def along_rows(self, tiles, root_col):
        ny, nk, nz, nx = self.shape
        slots = tiles.shape[0]
        z0, x0 = divmod(root_col, nx)
        rows = [(y, k) for y in range(ny) for k in range(nk)]
        assert slots == nx
        held = tiles[0]
        for j in range(1, nx):
            pairs = [((y, k, z0, x0), (y, k, z0, (x0 + j) % nx)) for y, k in rows]
            got, hit = self.send(tiles[j], pairs)
            held = jnp.where(hit, got, held)
        for sends in split_rounds(nz):
            results = []
            for offsets in sends:
                pairs = [
                    ((y, k, (z0 + a) % nz, x), (y, k, (z0 + b) % nz, x))
                    for y, k in rows
                    for x in range(nx)
                    for a, b in offsets
                ]
                results.append(self.send(held, pairs))
            for got, hit in results:
                held = jnp.where(hit, got, held)
        pieces = {0: held}
        left = held
        right = held
        for step in range(1, (nx - 1) // 2 + 2):
            if len(pieces) >= nx:
                break
            shift = [((y, k, z, x), (y, k, z, (x + 1) % nx)) for y, k in rows for z in range(nz) for x in range(nx)]
            left, _ = self.send(left, shift)
            pieces[-step] = left
            if len(pieces) >= nx:
                break
            shift = [((y, k, z, x), (y, k, z, (x - 1) % nx)) for y, k in rows for z in range(nz) for x in range(nx)]
            right, _ = self.send(right, shift)
            pieces[step] = right
        offsets = sorted(pieces)
        stack = jnp.stack([pieces[o] for o in offsets])
        base = (self.x - x0) % nx
        order = []
        for j in range(nx):
            pick = jnp.zeros((), jnp.int32)
            for i, o in enumerate(offsets):
                pick = jnp.where((base + o) % nx == j, i, pick)
            order.append(pick)
        return jnp.take(stack, jnp.stack(order), axis=0)


def solve_panel(factor, blocks):
    count = blocks.shape[0]
    width = blocks.shape[-1]
    stacked = jnp.transpose(blocks, (2, 0, 1)).reshape(width, count * width)
    solved = jax.scipy.linalg.solve_triangular(factor, stacked, lower=True)
    return jnp.transpose(solved.reshape(width, count, width), (1, 2, 0))


def products(rows, far):
    return jnp.einsum("sab,db->sad", rows, far, precision=lax.Precision.HIGHEST)


def make_on_device(shape):
    def on_device(matrix, present, update):
        g = Grid(shape)
        tiles = matrix[:, 0, 0]
        listed = present[:, 0, 0].astype(jnp.float32)
        flags = update[:, :, 0, 0].astype(jnp.float32)
        width = tiles.shape[-1]
        slots = tiles.shape[0]
        n_row, n_col = g.n_row, g.n_col
        identity = jnp.eye(width, dtype=jnp.float32)
        far_slot = g.col // n_row
        far_root = {c: c % n_row for c in range(2, n_col)}

        rows = [(y, k) for y in range(shape[0]) for k in range(shape[1])]
        a_row0, _ = g.send(tiles, [((y, k, 0, 0), (y, k, 0, 1)) for y, k in rows])
        got, hit = g.send(tiles[0], [((0, 0, 0, 0), (0, 0, 0, 1))])
        a00 = g.down_columns(jnp.where(hit, got, tiles[0]), {0: 0, 1: 0})
        a00, a_row0 = lax.optimization_barrier((a00, a_row0))

        owner0 = (g.row == 0) & (g.col == 0)
        second = g.col == 1
        factor0 = jnp.linalg.cholesky(jnp.where((g.col == 0) | second, a00, identity))
        source0 = jnp.where(second, a_row0, tiles)
        p0 = lax.cond((g.col == 0) | second, lambda d: solve_panel(factor0, d), lambda d: d, source0)
        p0 = p0.at[0].set(jnp.where(owner0, factor0, p0[0]))

        head = p0[1 // n_row]
        work11 = tiles[0] - flags[0, 0] * products(head[None], head)[0]
        owner1 = (g.row == 1) & second
        factor1 = jnp.linalg.cholesky(jnp.where(owner1, work11, identity))
        sent = g.down_columns(jnp.stack([factor1, head]), {1: 1 % n_row})
        work1 = tiles - flags[0][:, None, None] * products(p0, sent[1])
        p1 = lax.cond(second, lambda d: solve_panel(sent[0], d), lambda d: d, work1)
        p1 = p1.at[0].set(jnp.where(owner1, factor1, p1[0]))
        r01 = p0

        both = jnp.stack([r01, p1], axis=1)
        rows_both = g.along_rows(both, 1)
        far = g.down_columns(lax.dynamic_index_in_dim(rows_both, far_slot, 0, keepdims=False), far_root)
        rest = (tiles - flags[0][:, None, None] * products(rows_both[:, 0], far[0])) - flags[1][
            :, None, None
        ] * products(rows_both[:, 1], far[1])
        out = jnp.where(g.col == 0, p0, jnp.where(g.col == 1, p1, rest))
        return (out * listed[:, None, None])[:, None, None]

    return on_device


def solution(mesh):
    n_row = mesh.shape["row"]
    n_col = mesh.shape["col"]
    shape = (n_row // 2, 2, n_col // 4, 4)
    finer = Mesh(mesh.devices.reshape(shape), AXES)
    return jax.shard_map(
        make_on_device(shape),
        mesh=finer,
        in_specs=(P(None, ROW, COL, None, None), P(None, ROW, COL), P(None, None, ROW, COL)),
        out_specs=P(None, ROW, COL, None, None),
        check_vma=False,
    )
```

```python
import numpy as np
import jax
import jax.numpy as jnp
from jax import lax
from jax.sharding import Mesh
from jax.sharding import PartitionSpec as P

AXES = ("y", "core", "z", "x")
ROW = ("y", "core")
COL = ("z", "x")


def split_rounds(n, fan=1):
    spans = [(0, n)]
    rounds = []
    while any(length > 1 for _, length in spans):
        sends = [[] for _ in range(fan)]
        next_spans = []
        for start, length in spans:
            parts = min(fan + 1, length)
            sizes = [length // parts + (1 if i < length % parts else 0) for i in range(parts)]
            offset = start
            for i, size in enumerate(sizes):
                if i > 0:
                    sends[i - 1].append((start, offset))
                next_spans.append((offset, size))
                offset += size
        rounds.append([s for s in sends if s])
        spans = next_spans
    return rounds


class Grid:
    def __init__(self, shape):
        self.shape = shape
        ny, nk, nz, nx = shape
        self.n_row = ny * nk
        self.n_col = nz * nx
        self.y = lax.axis_index("y")
        self.core = lax.axis_index("core")
        self.z = lax.axis_index("z")
        self.x = lax.axis_index("x")
        self.row = self.y * nk + self.core
        self.col = self.z * nx + self.x
        self.lin = ((self.y * nk + self.core) * nz + self.z) * nx + self.x

    def index(self, y, k, z, x):
        ny, nk, nz, nx = self.shape
        return ((y * nk + k) * nz + z) * nx + x

    def send(self, value, pairs):
        perm = [(self.index(*s), self.index(*d)) for s, d in pairs]
        got = lax.ppermute(value, AXES, perm)
        mask = np.zeros(int(np.prod(self.shape)), bool)
        mask[[d for _, d in perm]] = True
        hit = jnp.asarray(mask)[self.lin]
        return got, hit

    def down_columns(self, value, roots):
        ny, nk, nz, nx = self.shape
        pairs = []
        for c, r in roots.items():
            z, x = divmod(c, nx)
            y0, k0 = divmod(r, nk)
            for k in range(nk):
                if k != k0:
                    pairs.append(((y0, k0, z, x), (y0, k, z, x)))
        if pairs:
            got, hit = self.send(value, pairs)
            value = jnp.where(hit, got, value)
        for sends in split_rounds(ny):
            results = []
            for offsets in sends:
                pairs = []
                for c, r in roots.items():
                    z, x = divmod(c, nx)
                    y0 = r // nk
                    for a, b in offsets:
                        for k in range(nk):
                            pairs.append((((y0 + a) % ny, k, z, x), ((y0 + b) % ny, k, z, x)))
                results.append(self.send(value, pairs))
            for got, hit in results:
                value = jnp.where(hit, got, value)
        return value

    def along_rows(self, tiles, root_col):
        ny, nk, nz, nx = self.shape
        slots = tiles.shape[0]
        z0, x0 = divmod(root_col, nx)
        rows = [(y, k) for y in range(ny) for k in range(nk)]
        assert slots == nx
        held = tiles[0]
        for j in range(1, nx):
            pairs = [((y, k, z0, x0), (y, k, z0, (x0 + j) % nx)) for y, k in rows]
            got, hit = self.send(tiles[j], pairs)
            held = jnp.where(hit, got, held)
        for sends in split_rounds(nz):
            results = []
            for offsets in sends:
                pairs = [
                    ((y, k, (z0 + a) % nz, x), (y, k, (z0 + b) % nz, x))
                    for y, k in rows
                    for x in range(nx)
                    for a, b in offsets
                ]
                results.append(self.send(held, pairs))
            for got, hit in results:
                held = jnp.where(hit, got, held)
        pieces = {0: held}
        left = held
        right = held
        for step in range(1, (nx - 1) // 2 + 2):
            if len(pieces) >= nx:
                break
            shift = [((y, k, z, x), (y, k, z, (x + 1) % nx)) for y, k in rows for z in range(nz) for x in range(nx)]
            left, _ = self.send(left, shift)
            pieces[-step] = left
            if len(pieces) >= nx:
                break
            shift = [((y, k, z, x), (y, k, z, (x - 1) % nx)) for y, k in rows for z in range(nz) for x in range(nx)]
            right, _ = self.send(right, shift)
            pieces[step] = right
        offsets = sorted(pieces)
        stack = jnp.stack([pieces[o] for o in offsets])
        base = (self.x - x0) % nx
        order = []
        for j in range(nx):
            pick = jnp.zeros((), jnp.int32)
            for i, o in enumerate(offsets):
                pick = jnp.where((base + o) % nx == j, i, pick)
            order.append(pick)
        return jnp.take(stack, jnp.stack(order), axis=0)


def solve_panel(factor, blocks):
    count = blocks.shape[0]
    width = blocks.shape[-1]
    stacked = jnp.transpose(blocks, (2, 0, 1)).reshape(width, count * width)
    solved = jax.scipy.linalg.solve_triangular(factor, stacked, lower=True)
    return jnp.transpose(solved.reshape(width, count, width), (1, 2, 0))


def products(rows, far):
    return jnp.einsum("sab,db->sad", rows, far, precision=lax.Precision.HIGHEST)


def make_on_device(shape):
    def on_device(matrix, present, update):
        g = Grid(shape)
        tiles = matrix[:, 0, 0]
        listed = present[:, 0, 0].astype(jnp.float32)
        flags = update[:, :, 0, 0].astype(jnp.float32)
        width = tiles.shape[-1]
        slots = tiles.shape[0]
        n_row, n_col = g.n_row, g.n_col
        identity = jnp.eye(width, dtype=jnp.float32)
        far_slot = g.col // n_row
        far_root = {c: c % n_row for c in range(2, n_col)}

        rows = [(y, k) for y in range(shape[0]) for k in range(shape[1])]
        a_row0, _ = g.send(tiles, [((y, k, 0, 0), (y, k, 0, 1)) for y, k in rows])
        got, hit = g.send(tiles[0], [((0, 0, 0, 0), (0, 0, 0, 1))])
        a00 = g.down_columns(jnp.where(hit, got, tiles[0]), {0: 0, 1: 0})
        a00, a_row0 = lax.optimization_barrier((a00, a_row0))

        owner0 = (g.row == 0) & (g.col == 0)
        second = g.col == 1
        factor0 = jnp.linalg.cholesky(jnp.where((g.col == 0) | second, a00, identity))
        source0 = jnp.where(second, a_row0, tiles)
        p0 = solve_panel(factor0, source0)
        p0 = p0.at[0].set(jnp.where(owner0, factor0, p0[0]))

        head = p0[1 // n_row]
        work11 = tiles[0] - flags[0, 0] * products(head[None], head)[0]
        owner1 = (g.row == 1) & second
        factor1 = jnp.linalg.cholesky(jnp.where(owner1, work11, identity))
        sent = g.down_columns(jnp.stack([factor1, head]), {1: 1 % n_row})
        work1 = tiles - flags[0][:, None, None] * products(p0, sent[1])
        p1 = solve_panel(sent[0], work1)
        p1 = p1.at[0].set(jnp.where(owner1, factor1, p1[0]))
        r01 = p0

        both = jnp.stack([r01, p1], axis=1)
        rows_both = g.along_rows(both, 1)
        far = g.down_columns(lax.dynamic_index_in_dim(rows_both, far_slot, 0, keepdims=False), far_root)
        rest = (tiles - flags[0][:, None, None] * products(rows_both[:, 0], far[0])) - flags[1][
            :, None, None
        ] * products(rows_both[:, 1], far[1])
        out = jnp.where(g.col == 0, p0, jnp.where(g.col == 1, p1, rest))
        return (out * listed[:, None, None])[:, None, None]

    return on_device


def solution(mesh):
    n_row = mesh.shape["row"]
    n_col = mesh.shape["col"]
    shape = (n_row // 2, 2, n_col // 4, 4)
    finer = Mesh(mesh.devices.reshape(shape), AXES)
    return jax.shard_map(
        make_on_device(shape),
        mesh=finer,
        in_specs=(P(None, ROW, COL, None, None), P(None, ROW, COL), P(None, None, ROW, COL)),
        out_specs=P(None, ROW, COL, None, None),
        check_vma=False,
    )
```

```python
import numpy as np
import jax
import jax.numpy as jnp
from jax import lax
from jax.sharding import Mesh
from jax.sharding import PartitionSpec as P

AXES = ("y", "core", "z", "x")
ROW = ("y", "core")
COL = ("z", "x")


def split_rounds(n, fan=1):
    spans = [(0, n)]
    rounds = []
    while any(length > 1 for _, length in spans):
        sends = [[] for _ in range(fan)]
        next_spans = []
        for start, length in spans:
            parts = min(fan + 1, length)
            sizes = [length // parts + (1 if i < length % parts else 0) for i in range(parts)]
            offset = start
            for i, size in enumerate(sizes):
                if i > 0:
                    sends[i - 1].append((start, offset))
                next_spans.append((offset, size))
                offset += size
        rounds.append([s for s in sends if s])
        spans = next_spans
    return rounds


class Grid:
    def __init__(self, shape):
        self.shape = shape
        ny, nk, nz, nx = shape
        self.n_row = ny * nk
        self.n_col = nz * nx
        self.y = lax.axis_index("y")
        self.core = lax.axis_index("core")
        self.z = lax.axis_index("z")
        self.x = lax.axis_index("x")
        self.row = self.y * nk + self.core
        self.col = self.z * nx + self.x
        self.lin = ((self.y * nk + self.core) * nz + self.z) * nx + self.x

    def index(self, y, k, z, x):
        ny, nk, nz, nx = self.shape
        return ((y * nk + k) * nz + z) * nx + x

    def send(self, value, pairs):
        perm = [(self.index(*s), self.index(*d)) for s, d in pairs]
        got = lax.ppermute(value, AXES, perm)
        mask = np.zeros(int(np.prod(self.shape)), bool)
        mask[[d for _, d in perm]] = True
        hit = jnp.asarray(mask)[self.lin]
        return got, hit

    def down_columns(self, value, roots):
        ny, nk, nz, nx = self.shape
        pairs = []
        for c, r in roots.items():
            z, x = divmod(c, nx)
            y0, k0 = divmod(r, nk)
            for k in range(nk):
                if k != k0:
                    pairs.append(((y0, k0, z, x), (y0, k, z, x)))
        if pairs:
            got, hit = self.send(value, pairs)
            value = jnp.where(hit, got, value)
        for sends in split_rounds(ny):
            results = []
            for offsets in sends:
                pairs = []
                for c, r in roots.items():
                    z, x = divmod(c, nx)
                    y0 = r // nk
                    for a, b in offsets:
                        for k in range(nk):
                            pairs.append((((y0 + a) % ny, k, z, x), ((y0 + b) % ny, k, z, x)))
                results.append(self.send(value, pairs))
            for got, hit in results:
                value = jnp.where(hit, got, value)
        return value

    def along_rows(self, tiles, root_col):
        ny, nk, nz, nx = self.shape
        slots = tiles.shape[0]
        z0, x0 = divmod(root_col, nx)
        rows = [(y, k) for y in range(ny) for k in range(nk)]
        assert slots == nx
        held = tiles[0]
        for j in range(1, nx):
            pairs = [((y, k, z0, x0), (y, k, z0, (x0 + j) % nx)) for y, k in rows]
            got, hit = self.send(tiles[j], pairs)
            held = jnp.where(hit, got, held)
        for sends in split_rounds(nz):
            results = []
            for offsets in sends:
                pairs = [
                    ((y, k, (z0 + a) % nz, x), (y, k, (z0 + b) % nz, x))
                    for y, k in rows
                    for x in range(nx)
                    for a, b in offsets
                ]
                results.append(self.send(held, pairs))
            for got, hit in results:
                held = jnp.where(hit, got, held)
        pieces = {0: held}
        for d in range(1, nx):
            shift = [((y, k, z, x), (y, k, z, (x + d) % nx)) for y, k in rows for z in range(nz) for x in range(nx)]
            pieces[-d], _ = self.send(held, shift)
        offsets = sorted(pieces)
        stack = jnp.stack([pieces[o] for o in offsets])
        base = (self.x - x0) % nx
        order = []
        for j in range(nx):
            pick = jnp.zeros((), jnp.int32)
            for i, o in enumerate(offsets):
                pick = jnp.where((base + o) % nx == j, i, pick)
            order.append(pick)
        return jnp.take(stack, jnp.stack(order), axis=0)


def solve_panel(factor, blocks):
    count = blocks.shape[0]
    width = blocks.shape[-1]
    stacked = jnp.transpose(blocks, (2, 0, 1)).reshape(width, count * width)
    solved = jax.scipy.linalg.solve_triangular(factor, stacked, lower=True)
    return jnp.transpose(solved.reshape(width, count, width), (1, 2, 0))


def products(rows, far):
    return jnp.einsum("sab,db->sad", rows, far, precision=lax.Precision.HIGHEST)


def make_on_device(shape):
    def on_device(matrix, present, update):
        g = Grid(shape)
        tiles = matrix[:, 0, 0]
        listed = present[:, 0, 0].astype(jnp.float32)
        flags = update[:, :, 0, 0].astype(jnp.float32)
        width = tiles.shape[-1]
        slots = tiles.shape[0]
        n_row, n_col = g.n_row, g.n_col
        identity = jnp.eye(width, dtype=jnp.float32)
        far_slot = g.col // n_row
        far_root = {c: c % n_row for c in range(2, n_col)}

        rows = [(y, k) for y in range(shape[0]) for k in range(shape[1])]
        a_row0, _ = g.send(tiles, [((y, k, 0, 0), (y, k, 0, 1)) for y, k in rows])
        got, hit = g.send(tiles[0], [((0, 0, 0, 0), (0, 0, 0, 1))])
        a00 = g.down_columns(jnp.where(hit, got, tiles[0]), {0: 0, 1: 0})
        a00, a_row0 = lax.optimization_barrier((a00, a_row0))

        owner0 = (g.row == 0) & (g.col == 0)
        second = g.col == 1
        factor0 = jnp.linalg.cholesky(jnp.where((g.col == 0) | second, a00, identity))
        source0 = jnp.where(second, a_row0, tiles)
        p0 = solve_panel(factor0, source0)
        p0 = p0.at[0].set(jnp.where(owner0, factor0, p0[0]))

        head = p0[1 // n_row]
        work11 = tiles[0] - flags[0, 0] * products(head[None], head)[0]
        owner1 = (g.row == 1) & second
        factor1 = jnp.linalg.cholesky(jnp.where(owner1, work11, identity))
        sent = g.down_columns(jnp.stack([factor1, head]), {1: 1 % n_row})
        work1 = tiles - flags[0][:, None, None] * products(p0, sent[1])
        p1 = solve_panel(sent[0], work1)
        p1 = p1.at[0].set(jnp.where(owner1, factor1, p1[0]))
        r01 = p0

        both = jnp.stack([r01, p1], axis=1)
        rows_both = g.along_rows(both, 1)
        far = g.down_columns(lax.dynamic_index_in_dim(rows_both, far_slot, 0, keepdims=False), far_root)
        rest = (tiles - flags[0][:, None, None] * products(rows_both[:, 0], far[0])) - flags[1][
            :, None, None
        ] * products(rows_both[:, 1], far[1])
        out = jnp.where(g.col == 0, p0, jnp.where(g.col == 1, p1, rest))
        return (out * listed[:, None, None])[:, None, None]

    return on_device


def solution(mesh):
    n_row = mesh.shape["row"]
    n_col = mesh.shape["col"]
    shape = (n_row // 2, 2, n_col // 4, 4)
    finer = Mesh(mesh.devices.reshape(shape), AXES)
    return jax.shard_map(
        make_on_device(shape),
        mesh=finer,
        in_specs=(P(None, ROW, COL, None, None), P(None, ROW, COL), P(None, None, ROW, COL)),
        out_specs=P(None, ROW, COL, None, None),
        check_vma=False,
    )
```

```python
import numpy as np
import jax
import jax.numpy as jnp
from jax import lax
from jax.sharding import Mesh
from jax.sharding import PartitionSpec as P

AXES = ("y", "core", "z", "x")
ROW = ("y", "core")
COL = ("z", "x")


def split_rounds(n, fan=1):
    spans = [(0, n)]
    rounds = []
    while any(length > 1 for _, length in spans):
        sends = [[] for _ in range(fan)]
        next_spans = []
        for start, length in spans:
            parts = min(fan + 1, length)
            sizes = [length // parts + (1 if i < length % parts else 0) for i in range(parts)]
            offset = start
            for i, size in enumerate(sizes):
                if i > 0:
                    sends[i - 1].append((start, offset))
                next_spans.append((offset, size))
                offset += size
        rounds.append([s for s in sends if s])
        spans = next_spans
    return rounds


class Grid:
    def __init__(self, shape):
        self.shape = shape
        ny, nk, nz, nx = shape
        self.n_row = ny * nk
        self.n_col = nz * nx
        self.y = lax.axis_index("y")
        self.core = lax.axis_index("core")
        self.z = lax.axis_index("z")
        self.x = lax.axis_index("x")
        self.row = self.y * nk + self.core
        self.col = self.z * nx + self.x
        self.lin = ((self.y * nk + self.core) * nz + self.z) * nx + self.x

    def index(self, y, k, z, x):
        ny, nk, nz, nx = self.shape
        return ((y * nk + k) * nz + z) * nx + x

    def send(self, value, pairs):
        perm = [(self.index(*s), self.index(*d)) for s, d in pairs]
        got = lax.ppermute(value, AXES, perm)
        mask = np.zeros(int(np.prod(self.shape)), bool)
        mask[[d for _, d in perm]] = True
        hit = jnp.asarray(mask)[self.lin]
        return got, hit

    def down_columns(self, value, roots):
        ny, nk, nz, nx = self.shape
        pairs = []
        for c, r in roots.items():
            z, x = divmod(c, nx)
            y0, k0 = divmod(r, nk)
            for k in range(nk):
                if k != k0:
                    pairs.append(((y0, k0, z, x), (y0, k, z, x)))
        if pairs:
            got, hit = self.send(value, pairs)
            value = jnp.where(hit, got, value)
        for sends in split_rounds(ny):
            results = []
            for offsets in sends:
                pairs = []
                for c, r in roots.items():
                    z, x = divmod(c, nx)
                    y0 = r // nk
                    for a, b in offsets:
                        for k in range(nk):
                            s = 1 - 2 * (k % 2)
                            pairs.append((((y0 + s * a) % ny, k, z, x), ((y0 + s * b) % ny, k, z, x)))
                results.append(self.send(value, pairs))
            for got, hit in results:
                value = jnp.where(hit, got, value)
        return value

    def along_rows(self, tiles, root_col):
        ny, nk, nz, nx = self.shape
        slots = tiles.shape[0]
        z0, x0 = divmod(root_col, nx)
        rows = [(y, k) for y in range(ny) for k in range(nk)]
        assert slots == nx
        held = tiles[0]
        for j in range(1, nx):
            pairs = [((y, k, z0, x0), (y, k, z0, (x0 + j) % nx)) for y, k in rows]
            got, hit = self.send(tiles[j], pairs)
            held = jnp.where(hit, got, held)
        for sends in split_rounds(nz):
            results = []
            for offsets in sends:
                pairs = [
                    ((y, k, (z0 + (1 - 2 * (k % 2)) * a) % nz, x), (y, k, (z0 + (1 - 2 * (k % 2)) * b) % nz, x))
                    for y, k in rows
                    for x in range(nx)
                    for a, b in offsets
                ]
                results.append(self.send(held, pairs))
            for got, hit in results:
                held = jnp.where(hit, got, held)
        pieces = {0: held}
        left = held
        right = held
        for step in range(1, (nx - 1) // 2 + 2):
            if len(pieces) >= nx:
                break
            shift = [((y, k, z, x), (y, k, z, (x + 1 - 2 * (k % 2)) % nx)) for y, k in rows for z in range(nz) for x in range(nx)]
            left, _ = self.send(left, shift)
            pieces[-step] = left
            if len(pieces) >= nx:
                break
            shift = [((y, k, z, x), (y, k, z, (x - 1 + 2 * (k % 2)) % nx)) for y, k in rows for z in range(nz) for x in range(nx)]
            right, _ = self.send(right, shift)
            pieces[step] = right
        offsets = sorted(pieces)
        stack = jnp.stack([pieces[o] for o in offsets])
        base = (self.x - x0) % nx
        order = []
        for j in range(nx):
            pick = jnp.zeros((), jnp.int32)
            for i, o in enumerate(offsets):
                pick = jnp.where((base + (1 - 2 * (self.core % 2)) * o) % nx == j, i, pick)
            order.append(pick)
        return jnp.take(stack, jnp.stack(order), axis=0)


def solve_panel(factor, blocks):
    count = blocks.shape[0]
    width = blocks.shape[-1]
    stacked = jnp.transpose(blocks, (2, 0, 1)).reshape(width, count * width)
    solved = jax.scipy.linalg.solve_triangular(factor, stacked, lower=True)
    return jnp.transpose(solved.reshape(width, count, width), (1, 2, 0))


def products(rows, far):
    return jnp.einsum("sab,db->sad", rows, far, precision=lax.Precision.HIGHEST)


def make_on_device(shape):
    def on_device(matrix, present, update):
        g = Grid(shape)
        tiles = matrix[:, 0, 0]
        listed = present[:, 0, 0].astype(jnp.float32)
        flags = update[:, :, 0, 0].astype(jnp.float32)
        width = tiles.shape[-1]
        slots = tiles.shape[0]
        n_row, n_col = g.n_row, g.n_col
        identity = jnp.eye(width, dtype=jnp.float32)
        far_slot = g.col // n_row
        far_root = {c: c % n_row for c in range(2, n_col)}

        rows = [(y, k) for y in range(shape[0]) for k in range(shape[1])]
        a_row0, _ = g.send(tiles, [((y, k, 0, 0), (y, k, 0, 1)) for y, k in rows])
        got, hit = g.send(tiles[0], [((0, 0, 0, 0), (0, 0, 0, 1))])
        a00 = g.down_columns(jnp.where(hit, got, tiles[0]), {0: 0, 1: 0})
        a00, a_row0 = lax.optimization_barrier((a00, a_row0))

        owner0 = (g.row == 0) & (g.col == 0)
        second = g.col == 1
        factor0 = jnp.linalg.cholesky(jnp.where((g.col == 0) | second, a00, identity))
        source0 = jnp.where(second, a_row0, tiles)
        p0 = solve_panel(factor0, source0)
        p0 = p0.at[0].set(jnp.where(owner0, factor0, p0[0]))

        head = p0[1 // n_row]
        work11 = tiles[0] - flags[0, 0] * products(head[None], head)[0]
        owner1 = (g.row == 1) & second
        factor1 = jnp.linalg.cholesky(jnp.where(owner1, work11, identity))
        sent = g.down_columns(jnp.stack([factor1, head]), {1: 1 % n_row})
        work1 = tiles - flags[0][:, None, None] * products(p0, sent[1])
        p1 = solve_panel(sent[0], work1)
        p1 = p1.at[0].set(jnp.where(owner1, factor1, p1[0]))
        r01 = p0

        both = jnp.stack([r01, p1], axis=1)
        rows_both = g.along_rows(both, 1)
        far = g.down_columns(lax.dynamic_index_in_dim(rows_both, far_slot, 0, keepdims=False), far_root)
        rest = (tiles - flags[0][:, None, None] * products(rows_both[:, 0], far[0])) - flags[1][
            :, None, None
        ] * products(rows_both[:, 1], far[1])
        out = jnp.where(g.col == 0, p0, jnp.where(g.col == 1, p1, rest))
        return (out * listed[:, None, None])[:, None, None]

    return on_device


def solution(mesh):
    n_row = mesh.shape["row"]
    n_col = mesh.shape["col"]
    shape = (n_row // 2, 2, n_col // 4, 4)
    finer = Mesh(mesh.devices.reshape(shape), AXES)
    return jax.shard_map(
        make_on_device(shape),
        mesh=finer,
        in_specs=(P(None, ROW, COL, None, None), P(None, ROW, COL), P(None, None, ROW, COL)),
        out_specs=P(None, ROW, COL, None, None),
        check_vma=False,
    )
```

```python
import numpy as np
import jax
import jax.numpy as jnp
from jax import lax
from jax.sharding import Mesh
from jax.sharding import PartitionSpec as P

AXES = ("y", "core", "z", "x")
ROW = ("y", "core")
COL = ("z", "x")


def split_rounds(n, fan=1):
    spans = [(0, n)]
    rounds = []
    while any(length > 1 for _, length in spans):
        sends = [[] for _ in range(fan)]
        next_spans = []
        for start, length in spans:
            parts = min(fan + 1, length)
            sizes = [length // parts + (1 if i < length % parts else 0) for i in range(parts)]
            offset = start
            for i, size in enumerate(sizes):
                if i > 0:
                    sends[i - 1].append((start, offset))
                next_spans.append((offset, size))
                offset += size
        rounds.append([s for s in sends if s])
        spans = next_spans
    return rounds


class Grid:
    def __init__(self, shape):
        self.shape = shape
        ny, nk, nz, nx = shape
        self.n_row = ny * nk
        self.n_col = nz * nx
        self.y = lax.axis_index("y")
        self.core = lax.axis_index("core")
        self.z = lax.axis_index("z")
        self.x = lax.axis_index("x")
        self.row = self.y * nk + self.core
        self.col = self.z * nx + self.x
        self.lin = ((self.y * nk + self.core) * nz + self.z) * nx + self.x

    def index(self, y, k, z, x):
        ny, nk, nz, nx = self.shape
        return ((y * nk + k) * nz + z) * nx + x

    def send(self, value, pairs):
        perm = [(self.index(*s), self.index(*d)) for s, d in pairs]
        got = lax.ppermute(value, AXES, perm)
        mask = np.zeros(int(np.prod(self.shape)), bool)
        mask[[d for _, d in perm]] = True
        hit = jnp.asarray(mask)[self.lin]
        return got, hit

    def down_columns(self, value, roots):
        ny, nk, nz, nx = self.shape
        pairs = []
        for c, r in roots.items():
            z, x = divmod(c, nx)
            y0, k0 = divmod(r, nk)
            for k in range(nk):
                if k != k0:
                    pairs.append(((y0, k0, z, x), (y0, k, z, x)))
        if pairs:
            got, hit = self.send(value, pairs)
            value = jnp.where(hit, got, value)
        for sends in split_rounds(ny):
            results = []
            for offsets in sends:
                pairs = []
                for c, r in roots.items():
                    z, x = divmod(c, nx)
                    y0 = r // nk
                    for a, b in offsets:
                        for k in range(nk):
                            s = 1 - 2 * (k % 2)
                            pairs.append((((y0 + s * a) % ny, k, z, x), ((y0 + s * b) % ny, k, z, x)))
                results.append(self.send(value, pairs))
            for got, hit in results:
                value = jnp.where(hit, got, value)
        return value

    def along_rows(self, tiles, root_col):
        ny, nk, nz, nx = self.shape
        slots = tiles.shape[0]
        z0, x0 = divmod(root_col, nx)
        rows = [(y, k) for y in range(ny) for k in range(nk)]
        assert slots == nx
        held = tiles[0]
        for j in range(1, nx):
            pairs = [((y, k, z0, x0), (y, k, z0, (x0 + (1 - 2 * (k % 2)) * j) % nx)) for y, k in rows]
            got, hit = self.send(tiles[j], pairs)
            held = jnp.where(hit, got, held)
        for sends in split_rounds(nz):
            results = []
            for offsets in sends:
                pairs = [
                    ((y, k, (z0 + (1 - 2 * (k % 2)) * a) % nz, x), (y, k, (z0 + (1 - 2 * (k % 2)) * b) % nz, x))
                    for y, k in rows
                    for x in range(nx)
                    for a, b in offsets
                ]
                results.append(self.send(held, pairs))
            for got, hit in results:
                held = jnp.where(hit, got, held)
        pieces = {0: held}
        left = held
        right = held
        for step in range(1, (nx - 1) // 2 + 2):
            if len(pieces) >= nx:
                break
            shift = [((y, k, z, x), (y, k, z, (x + 1 - 2 * (k % 2)) % nx)) for y, k in rows for z in range(nz) for x in range(nx)]
            left, _ = self.send(left, shift)
            pieces[-step] = left
            if len(pieces) >= nx:
                break
            shift = [((y, k, z, x), (y, k, z, (x - 1 + 2 * (k % 2)) % nx)) for y, k in rows for z in range(nz) for x in range(nx)]
            right, _ = self.send(right, shift)
            pieces[step] = right
        offsets = sorted(pieces)
        stack = jnp.stack([pieces[o] for o in offsets])
        base = ((1 - 2 * (self.core % 2)) * (self.x - x0)) % nx
        order = []
        for j in range(nx):
            pick = jnp.zeros((), jnp.int32)
            for i, o in enumerate(offsets):
                pick = jnp.where((base + o) % nx == j, i, pick)
            order.append(pick)
        return jnp.take(stack, jnp.stack(order), axis=0)


def solve_panel(factor, blocks):
    count = blocks.shape[0]
    width = blocks.shape[-1]
    stacked = jnp.transpose(blocks, (2, 0, 1)).reshape(width, count * width)
    solved = jax.scipy.linalg.solve_triangular(factor, stacked, lower=True)
    return jnp.transpose(solved.reshape(width, count, width), (1, 2, 0))


def products(rows, far):
    return jnp.einsum("sab,db->sad", rows, far, precision=lax.Precision.HIGHEST)


def make_on_device(shape):
    def on_device(matrix, present, update):
        g = Grid(shape)
        tiles = matrix[:, 0, 0]
        listed = present[:, 0, 0].astype(jnp.float32)
        flags = update[:, :, 0, 0].astype(jnp.float32)
        width = tiles.shape[-1]
        slots = tiles.shape[0]
        n_row, n_col = g.n_row, g.n_col
        identity = jnp.eye(width, dtype=jnp.float32)
        far_slot = g.col // n_row
        far_root = {c: c % n_row for c in range(2, n_col)}

        rows = [(y, k) for y in range(shape[0]) for k in range(shape[1])]
        a_row0, _ = g.send(tiles, [((y, k, 0, 0), (y, k, 0, 1)) for y, k in rows])
        got, hit = g.send(tiles[0], [((0, 0, 0, 0), (0, 0, 0, 1))])
        a00 = g.down_columns(jnp.where(hit, got, tiles[0]), {0: 0, 1: 0})
        a00, a_row0 = lax.optimization_barrier((a00, a_row0))

        owner0 = (g.row == 0) & (g.col == 0)
        second = g.col == 1
        factor0 = jnp.linalg.cholesky(jnp.where((g.col == 0) | second, a00, identity))
        source0 = jnp.where(second, a_row0, tiles)
        p0 = solve_panel(factor0, source0)
        p0 = p0.at[0].set(jnp.where(owner0, factor0, p0[0]))

        head = p0[1 // n_row]
        work11 = tiles[0] - flags[0, 0] * products(head[None], head)[0]
        owner1 = (g.row == 1) & second
        factor1 = jnp.linalg.cholesky(jnp.where(owner1, work11, identity))
        sent = g.down_columns(jnp.stack([factor1, head]), {1: 1 % n_row})
        work1 = tiles - flags[0][:, None, None] * products(p0, sent[1])
        p1 = solve_panel(sent[0], work1)
        p1 = p1.at[0].set(jnp.where(owner1, factor1, p1[0]))
        r01 = p0

        both = jnp.stack([r01, p1], axis=1)
        rows_both = g.along_rows(both, 1)
        far = g.down_columns(lax.dynamic_index_in_dim(rows_both, far_slot, 0, keepdims=False), far_root)
        rest = (tiles - flags[0][:, None, None] * products(rows_both[:, 0], far[0])) - flags[1][
            :, None, None
        ] * products(rows_both[:, 1], far[1])
        out = jnp.where(g.col == 0, p0, jnp.where(g.col == 1, p1, rest))
        return (out * listed[:, None, None])[:, None, None]

    return on_device


def solution(mesh):
    n_row = mesh.shape["row"]
    n_col = mesh.shape["col"]
    shape = (n_row // 2, 2, n_col // 4, 4)
    finer = Mesh(mesh.devices.reshape(shape), AXES)
    return jax.shard_map(
        make_on_device(shape),
        mesh=finer,
        in_specs=(P(None, ROW, COL, None, None), P(None, ROW, COL), P(None, None, ROW, COL)),
        out_specs=P(None, ROW, COL, None, None),
        check_vma=False,
    )
```

```python
import numpy as np
import jax
import jax.numpy as jnp
from jax import lax
from jax.sharding import Mesh
from jax.sharding import PartitionSpec as P

AXES = ("y", "core", "z", "x")
ROW = ("y", "core")
COL = ("z", "x")


def split_rounds(n, fan=1, cut=None):
    spans = [(0, n)]
    rounds = []
    if cut is not None and 0 < cut < n:
        rest = split_rounds(n - cut, fan)
        head = split_rounds(cut, fan)
        rounds.append([[(0, cut)]])
        for i in range(max(len(rest), len(head))):
            a = head[i] if i < len(head) else []
            b = [[(s + cut, d + cut) for s, d in lst] for lst in rest[i]] if i < len(rest) else []
            rounds.append([x + y for x, y in zip(a, b)] + a[len(b):] + b[len(a):])
        return rounds
    while any(length > 1 for _, length in spans):
        sends = [[] for _ in range(fan)]
        next_spans = []
        for start, length in spans:
            parts = min(fan + 1, length)
            sizes = [length // parts + (1 if i < length % parts else 0) for i in range(parts)]
            offset = start
            for i, size in enumerate(sizes):
                if i > 0:
                    sends[i - 1].append((start, offset))
                next_spans.append((offset, size))
                offset += size
        rounds.append([s for s in sends if s])
        spans = next_spans
    return rounds


class Grid:
    def __init__(self, shape):
        self.shape = shape
        ny, nk, nz, nx = shape
        self.n_row = ny * nk
        self.n_col = nz * nx
        self.y = lax.axis_index("y")
        self.core = lax.axis_index("core")
        self.z = lax.axis_index("z")
        self.x = lax.axis_index("x")
        self.row = self.y * nk + self.core
        self.col = self.z * nx + self.x
        self.lin = ((self.y * nk + self.core) * nz + self.z) * nx + self.x

    def index(self, y, k, z, x):
        ny, nk, nz, nx = self.shape
        return ((y * nk + k) * nz + z) * nx + x

    def send(self, value, pairs):
        perm = [(self.index(*s), self.index(*d)) for s, d in pairs]
        got = lax.ppermute(value, AXES, perm)
        mask = np.zeros(int(np.prod(self.shape)), bool)
        mask[[d for _, d in perm]] = True
        hit = jnp.asarray(mask)[self.lin]
        return got, hit

    def down_columns(self, value, roots):
        ny, nk, nz, nx = self.shape
        pairs = []
        for c, r in roots.items():
            z, x = divmod(c, nx)
            y0, k0 = divmod(r, nk)
            for k in range(nk):
                if k != k0:
                    pairs.append(((y0, k0, z, x), (y0, k, z, x)))
        if pairs:
            got, hit = self.send(value, pairs)
            value = jnp.where(hit, got, value)
        for sends in split_rounds(ny):
            results = []
            for offsets in sends:
                pairs = []
                for c, r in roots.items():
                    z, x = divmod(c, nx)
                    y0 = r // nk
                    for a, b in offsets:
                        for k in range(nk):
                            s = 1 - 2 * (k % 2)
                            pairs.append((((y0 + s * a) % ny, k, z, x), ((y0 + s * b) % ny, k, z, x)))
                results.append(self.send(value, pairs))
            for got, hit in results:
                value = jnp.where(hit, got, value)
        return value

    def along_rows(self, tiles, root_col):
        ny, nk, nz, nx = self.shape
        slots = tiles.shape[0]
        z0, x0 = divmod(root_col, nx)
        rows = [(y, k) for y in range(ny) for k in range(nk)]
        assert slots == nx
        held = tiles[0]
        for j in range(1, nx):
            pairs = [((y, k, z0, x0), (y, k, z0, (x0 + (1 - 2 * (k % 2)) * j) % nx)) for y, k in rows]
            got, hit = self.send(tiles[j], pairs)
            held = jnp.where(hit, got, held)
        plans = [split_rounds(nz), split_rounds(nz, cut=nz // 2 - 1)]
        if len(plans[1]) != len(plans[0]):
            plans[1] = plans[0]
        for level in range(len(plans[0])):
            results = []
            for i in range(max(len(p[level]) for p in plans)):
                pairs = []
                for y, k in rows:
                    plan, s = plans[k % 2], 1 - 2 * (k % 2)
                    if i < len(plan[level]):
                        for a, b in plan[level][i]:
                            pairs += [((y, k, (z0 + s * a) % nz, x), (y, k, (z0 + s * b) % nz, x)) for x in range(nx)]
                results.append(self.send(held, pairs))
            for got, hit in results:
                held = jnp.where(hit, got, held)
        pieces = {0: held}
        left = held
        right = held
        for step in range(1, (nx - 1) // 2 + 2):
            if len(pieces) >= nx:
                break
            shift = [((y, k, z, x), (y, k, z, (x + 1 - 2 * (k % 2)) % nx)) for y, k in rows for z in range(nz) for x in range(nx)]
            left, _ = self.send(left, shift)
            pieces[-step] = left
            if len(pieces) >= nx:
                break
            shift = [((y, k, z, x), (y, k, z, (x - 1 + 2 * (k % 2)) % nx)) for y, k in rows for z in range(nz) for x in range(nx)]
            right, _ = self.send(right, shift)
            pieces[step] = right
        offsets = sorted(pieces)
        stack = jnp.stack([pieces[o] for o in offsets])
        base = ((1 - 2 * (self.core % 2)) * (self.x - x0)) % nx
        order = []
        for j in range(nx):
            pick = jnp.zeros((), jnp.int32)
            for i, o in enumerate(offsets):
                pick = jnp.where((base + o) % nx == j, i, pick)
            order.append(pick)
        return jnp.take(stack, jnp.stack(order), axis=0)


def solve_panel(factor, blocks):
    count = blocks.shape[0]
    width = blocks.shape[-1]
    stacked = jnp.transpose(blocks, (2, 0, 1)).reshape(width, count * width)
    solved = jax.scipy.linalg.solve_triangular(factor, stacked, lower=True)
    return jnp.transpose(solved.reshape(width, count, width), (1, 2, 0))


def products(rows, far):
    return jnp.einsum("sab,db->sad", rows, far, precision=lax.Precision.HIGHEST)


def make_on_device(shape):
    def on_device(matrix, present, update):
        g = Grid(shape)
        tiles = matrix[:, 0, 0]
        listed = present[:, 0, 0].astype(jnp.float32)
        flags = update[:, :, 0, 0].astype(jnp.float32)
        width = tiles.shape[-1]
        slots = tiles.shape[0]
        n_row, n_col = g.n_row, g.n_col
        identity = jnp.eye(width, dtype=jnp.float32)
        far_slot = g.col // n_row
        far_root = {c: c % n_row for c in range(2, n_col)}

        rows = [(y, k) for y in range(shape[0]) for k in range(shape[1])]
        a_row0, _ = g.send(tiles, [((y, k, 0, 0), (y, k, 0, 1)) for y, k in rows])
        got, hit = g.send(tiles[0], [((0, 0, 0, 0), (0, 0, 0, 1))])
        a00 = g.down_columns(jnp.where(hit, got, tiles[0]), {0: 0, 1: 0})
        a00, a_row0 = lax.optimization_barrier((a00, a_row0))

        owner0 = (g.row == 0) & (g.col == 0)
        second = g.col == 1
        factor0 = jnp.linalg.cholesky(jnp.where((g.col == 0) | second, a00, identity))
        source0 = jnp.where(second, a_row0, tiles)
        p0 = solve_panel(factor0, source0)
        p0 = p0.at[0].set(jnp.where(owner0, factor0, p0[0]))

        head = p0[1 // n_row]
        work11 = tiles[0] - flags[0, 0] * products(head[None], head)[0]
        owner1 = (g.row == 1) & second
        factor1 = jnp.linalg.cholesky(jnp.where(owner1, work11, identity))
        sent = g.down_columns(jnp.stack([factor1, head]), {1: 1 % n_row})
        work1 = tiles - flags[0][:, None, None] * products(p0, sent[1])
        p1 = solve_panel(sent[0], work1)
        p1 = p1.at[0].set(jnp.where(owner1, factor1, p1[0]))
        r01 = p0

        both = jnp.stack([r01, p1], axis=1)
        rows_both = g.along_rows(both, 1)
        far = g.down_columns(lax.dynamic_index_in_dim(rows_both, far_slot, 0, keepdims=False), far_root)
        rest = (tiles - flags[0][:, None, None] * products(rows_both[:, 0], far[0])) - flags[1][
            :, None, None
        ] * products(rows_both[:, 1], far[1])
        out = jnp.where(g.col == 0, p0, jnp.where(g.col == 1, p1, rest))
        return (out * listed[:, None, None])[:, None, None]

    return on_device


def solution(mesh):
    n_row = mesh.shape["row"]
    n_col = mesh.shape["col"]
    shape = (n_row // 2, 2, n_col // 4, 4)
    finer = Mesh(mesh.devices.reshape(shape), AXES)
    return jax.shard_map(
        make_on_device(shape),
        mesh=finer,
        in_specs=(P(None, ROW, COL, None, None), P(None, ROW, COL), P(None, None, ROW, COL)),
        out_specs=P(None, ROW, COL, None, None),
        check_vma=False,
    )
```

```python
import numpy as np
import jax
import jax.numpy as jnp
from jax import lax
from jax.sharding import Mesh
from jax.sharding import PartitionSpec as P

AXES = ("y", "core", "z", "x")
ROW = ("y", "core")
COL = ("z", "x")


def split_rounds(n, fan=1, cut=None):
    spans = [(0, n)]
    rounds = []
    if cut is not None and 0 < cut < n:
        rest = split_rounds(n - cut, fan)
        head = split_rounds(cut, fan)
        rounds.append([[(0, cut)]])
        for i in range(max(len(rest), len(head))):
            a = head[i] if i < len(head) else []
            b = [[(s + cut, d + cut) for s, d in lst] for lst in rest[i]] if i < len(rest) else []
            rounds.append([x + y for x, y in zip(a, b)] + a[len(b):] + b[len(a):])
        return rounds
    while any(length > 1 for _, length in spans):
        sends = [[] for _ in range(fan)]
        next_spans = []
        for start, length in spans:
            parts = min(fan + 1, length)
            sizes = [length // parts + (1 if i < length % parts else 0) for i in range(parts)]
            offset = start
            for i, size in enumerate(sizes):
                if i > 0:
                    sends[i - 1].append((start, offset))
                next_spans.append((offset, size))
                offset += size
        rounds.append([s for s in sends if s])
        spans = next_spans
    return rounds


class Grid:
    def __init__(self, shape):
        self.shape = shape
        ny, nk, nz, nx = shape
        self.n_row = ny * nk
        self.n_col = nz * nx
        self.y = lax.axis_index("y")
        self.core = lax.axis_index("core")
        self.z = lax.axis_index("z")
        self.x = lax.axis_index("x")
        self.row = self.y * nk + self.core
        self.col = self.z * nx + self.x
        self.lin = ((self.y * nk + self.core) * nz + self.z) * nx + self.x

    def index(self, y, k, z, x):
        ny, nk, nz, nx = self.shape
        return ((y * nk + k) * nz + z) * nx + x

    def send(self, value, pairs):
        perm = [(self.index(*s), self.index(*d)) for s, d in pairs]
        got = lax.ppermute(value, AXES, perm)
        mask = np.zeros(int(np.prod(self.shape)), bool)
        mask[[d for _, d in perm]] = True
        hit = jnp.asarray(mask)[self.lin]
        return got, hit

    def down_columns(self, value, roots):
        ny, nk, nz, nx = self.shape
        pairs = []
        for c, r in roots.items():
            z, x = divmod(c, nx)
            y0, k0 = divmod(r, nk)
            for k in range(nk):
                if k != k0:
                    pairs.append(((y0, k0, z, x), (y0, k, z, x)))
        if pairs:
            got, hit = self.send(value, pairs)
            value = jnp.where(hit, got, value)
        for sends in split_rounds(ny):
            results = []
            for offsets in sends:
                pairs = []
                for c, r in roots.items():
                    z, x = divmod(c, nx)
                    y0 = r // nk
                    for a, b in offsets:
                        for k in range(nk):
                            s = 1 - 2 * (k % 2)
                            pairs.append((((y0 + s * a) % ny, k, z, x), ((y0 + s * b) % ny, k, z, x)))
                results.append(self.send(value, pairs))
            for got, hit in results:
                value = jnp.where(hit, got, value)
        return value

    def along_rows(self, tiles, root_col):
        ny, nk, nz, nx = self.shape
        slots = tiles.shape[0]
        z0, x0 = divmod(root_col, nx)
        rows = [(y, k) for y in range(ny) for k in range(nk)]
        assert slots == nx
        held = tiles[0]
        for j in range(1, nx):
            pairs = [((y, k, z0, x0), (y, k, z0, (x0 + (1 - 2 * (k % 2)) * j) % nx)) for y, k in rows]
            got, hit = self.send(tiles[j], pairs)
            held = jnp.where(hit, got, held)
        plans = [split_rounds(nz), split_rounds(nz, cut=nz // 2 - 1)]
        if len(plans[1]) != len(plans[0]):
            plans[1] = plans[0]
        for level in range(len(plans[0])):
            results = []
            for i in range(max(len(p[level]) for p in plans)):
                pairs = []
                for y, k in rows:
                    plan, s = plans[k % 2], 1 - 2 * (k % 2)
                    if i < len(plan[level]):
                        for a, b in plan[level][i]:
                            pairs += [((y, k, (z0 + s * a) % nz, x), (y, k, (z0 + s * b) % nz, x)) for x in range(nx)]
                results.append(self.send(held, pairs))
            for got, hit in results:
                held = jnp.where(hit, got, held)
        pieces = {0: held}
        left = held
        right = held
        for step in range(1, (nx - 1) // 2 + 2):
            if len(pieces) >= nx:
                break
            shift = [((y, k, z, x), (y, k, z, (x + 1 - 2 * (k % 2)) % nx)) for y, k in rows for z in range(nz) for x in range(nx)]
            left, _ = self.send(left, shift)
            pieces[-step] = left
            if len(pieces) >= nx:
                break
            shift = [((y, k, z, x), (y, k, z, (x - 1 + 2 * (k % 2)) % nx)) for y, k in rows for z in range(nz) for x in range(nx)]
            right, _ = self.send(right, shift)
            pieces[step] = right
        offsets = sorted(pieces)
        stack = jnp.stack([pieces[o] for o in offsets])
        base = ((1 - 2 * (self.core % 2)) * (self.x - x0)) % nx
        order = []
        for j in range(nx):
            pick = jnp.zeros((), jnp.int32)
            for i, o in enumerate(offsets):
                pick = jnp.where((base + o) % nx == j, i, pick)
            order.append(pick)
        return stack, jnp.stack(order)


def solve_panel(factor, blocks):
    count = blocks.shape[0]
    width = blocks.shape[-1]
    stacked = jnp.transpose(blocks, (2, 0, 1)).reshape(width, count * width)
    solved = jax.scipy.linalg.solve_triangular(factor, stacked, lower=True)
    return jnp.transpose(solved.reshape(width, count, width), (1, 2, 0))


def products(rows, far):
    return jnp.einsum("sab,db->sad", rows, far, precision=lax.Precision.HIGHEST)


def make_on_device(shape):
    def on_device(matrix, present, update):
        g = Grid(shape)
        tiles = matrix[:, 0, 0]
        listed = present[:, 0, 0].astype(jnp.float32)
        flags = update[:, :, 0, 0].astype(jnp.float32)
        width = tiles.shape[-1]
        slots = tiles.shape[0]
        n_row, n_col = g.n_row, g.n_col
        identity = jnp.eye(width, dtype=jnp.float32)
        far_slot = g.col // n_row
        far_root = {c: c % n_row for c in range(2, n_col)}

        rows = [(y, k) for y in range(shape[0]) for k in range(shape[1])]
        a_row0, _ = g.send(tiles, [((y, k, 0, 0), (y, k, 0, 1)) for y, k in rows])
        got, hit = g.send(tiles[0], [((0, 0, 0, 0), (0, 0, 0, 1))])
        a00 = g.down_columns(jnp.where(hit, got, tiles[0]), {0: 0, 1: 0})
        a00, a_row0 = lax.optimization_barrier((a00, a_row0))

        owner0 = (g.row == 0) & (g.col == 0)
        second = g.col == 1
        factor0 = jnp.linalg.cholesky(jnp.where((g.col == 0) | second, a00, identity))
        source0 = jnp.where(second, a_row0, tiles)
        p0 = solve_panel(factor0, source0)
        p0 = p0.at[0].set(jnp.where(owner0, factor0, p0[0]))

        head = p0[1 // n_row]
        work11 = tiles[0] - flags[0, 0] * products(head[None], head)[0]
        owner1 = (g.row == 1) & second
        factor1 = jnp.linalg.cholesky(jnp.where(owner1, work11, identity))
        sent = g.down_columns(jnp.stack([factor1, head]), {1: 1 % n_row})
        work1 = tiles - flags[0][:, None, None] * products(p0, sent[1])
        p1 = solve_panel(sent[0], work1)
        p1 = p1.at[0].set(jnp.where(owner1, factor1, p1[0]))
        r01 = p0

        both = jnp.stack([r01, p1], axis=1)
        stack, order = g.along_rows(both, 1)
        far_in = lax.dynamic_index_in_dim(stack, order[far_slot], 0, keepdims=False)
        far = g.down_columns(far_in, far_root)
        rows_both = jnp.take(stack, order, axis=0)
        rest = (tiles - flags[0][:, None, None] * products(rows_both[:, 0], far[0])) - flags[1][
            :, None, None
        ] * products(rows_both[:, 1], far[1])
        out = jnp.where(g.col == 0, p0, jnp.where(g.col == 1, p1, rest))
        return (out * listed[:, None, None])[:, None, None]

    return on_device


def solution(mesh):
    n_row = mesh.shape["row"]
    n_col = mesh.shape["col"]
    shape = (n_row // 2, 2, n_col // 4, 4)
    finer = Mesh(mesh.devices.reshape(shape), AXES)
    return jax.shard_map(
        make_on_device(shape),
        mesh=finer,
        in_specs=(P(None, ROW, COL, None, None), P(None, ROW, COL), P(None, None, ROW, COL)),
        out_specs=P(None, ROW, COL, None, None),
        check_vma=False,
    )
```

```python
import numpy as np
import jax
import jax.numpy as jnp
from jax import lax
from jax.sharding import Mesh
from jax.sharding import PartitionSpec as P

AXES = ("y", "core", "z", "x")
ROW = ("y", "core")
COL = ("z", "x")


def split_rounds(n, fan=1, cut=None):
    spans = [(0, n)]
    rounds = []
    if cut is not None and 0 < cut < n:
        rest = split_rounds(n - cut, fan)
        head = split_rounds(cut, fan)
        rounds.append([[(0, cut)]])
        for i in range(max(len(rest), len(head))):
            a = head[i] if i < len(head) else []
            b = [[(s + cut, d + cut) for s, d in lst] for lst in rest[i]] if i < len(rest) else []
            rounds.append([x + y for x, y in zip(a, b)] + a[len(b):] + b[len(a):])
        return rounds
    while any(length > 1 for _, length in spans):
        sends = [[] for _ in range(fan)]
        next_spans = []
        for start, length in spans:
            parts = min(fan + 1, length)
            sizes = [length // parts + (1 if i < length % parts else 0) for i in range(parts)]
            offset = start
            for i, size in enumerate(sizes):
                if i > 0:
                    sends[i - 1].append((start, offset))
                next_spans.append((offset, size))
                offset += size
        rounds.append([s for s in sends if s])
        spans = next_spans
    return rounds


class Grid:
    def __init__(self, shape):
        self.shape = shape
        ny, nk, nz, nx = shape
        self.n_row = ny * nk
        self.n_col = nz * nx
        self.y = lax.axis_index("y")
        self.core = lax.axis_index("core")
        self.z = lax.axis_index("z")
        self.x = lax.axis_index("x")
        self.row = self.y * nk + self.core
        self.col = self.z * nx + self.x
        self.lin = ((self.y * nk + self.core) * nz + self.z) * nx + self.x

    def index(self, y, k, z, x):
        ny, nk, nz, nx = self.shape
        return ((y * nk + k) * nz + z) * nx + x

    def send(self, value, pairs):
        perm = [(self.index(*s), self.index(*d)) for s, d in pairs]
        got = lax.ppermute(value, AXES, perm)
        mask = np.zeros(int(np.prod(self.shape)), bool)
        mask[[d for _, d in perm]] = True
        hit = jnp.asarray(mask)[self.lin]
        return got, hit

    def down_columns(self, value, roots):
        ny, nk, nz, nx = self.shape
        pairs = []
        for c, r in roots.items():
            z, x = divmod(c, nx)
            y0, k0 = divmod(r, nk)
            for k in range(nk):
                if k != k0:
                    pairs.append(((y0, k0, z, x), (y0, k, z, x)))
        if pairs:
            got, hit = self.send(value, pairs)
            value = jnp.where(hit, got, value)
        for sends in split_rounds(ny):
            results = []
            for offsets in sends:
                pairs = []
                for c, r in roots.items():
                    z, x = divmod(c, nx)
                    y0 = r // nk
                    for a, b in offsets:
                        for k in range(nk):
                            s = 1 - 2 * (k % 2)
                            pairs.append((((y0 + s * a) % ny, k, z, x), ((y0 + s * b) % ny, k, z, x)))
                results.append(self.send(value, pairs))
            for got, hit in results:
                value = jnp.where(hit, got, value)
        return value

    def along_rows(self, tiles, root_col):
        ny, nk, nz, nx = self.shape
        slots = tiles.shape[0]
        z0, x0 = divmod(root_col, nx)
        rows = [(y, k) for y in range(ny) for k in range(nk)]
        assert slots == nx
        held = tiles[0]
        for j in range(1, nx):
            pairs = [((y, k, z0, x0), (y, k, z0, (x0 + (1 - 2 * (k % 2)) * j) % nx)) for y, k in rows]
            got, hit = self.send(tiles[j], pairs)
            held = jnp.where(hit, got, held)
        plans = [split_rounds(nz), split_rounds(nz, cut=nz // 2 - 1)]
        if len(plans[1]) != len(plans[0]):
            plans[1] = plans[0]
        for level in range(len(plans[0])):
            results = []
            for i in range(max(len(p[level]) for p in plans)):
                pairs = []
                for y, k in rows:
                    plan, s = plans[k % 2], 1 - 2 * (k % 2)
                    if i < len(plan[level]):
                        for a, b in plan[level][i]:
                            pairs += [((y, k, (z0 + s * a) % nz, x), (y, k, (z0 + s * b) % nz, x)) for x in range(nx)]
                results.append(self.send(held, pairs))
            for got, hit in results:
                held = jnp.where(hit, got, held)
        pieces = {0: held}
        left = held
        right = held
        for step in range(1, (nx - 1) // 2 + 2):
            if len(pieces) >= nx:
                break
            shift = [((y, k, z, x), (y, k, z, (x + 1 - 2 * (k % 2)) % nx)) for y, k in rows for z in range(nz) for x in range(nx)]
            left, _ = self.send(left, shift)
            pieces[-step] = left
            if len(pieces) >= nx:
                break
            shift = [((y, k, z, x), (y, k, z, (x - 1 + 2 * (k % 2)) % nx)) for y, k in rows for z in range(nz) for x in range(nx)]
            right, _ = self.send(right, shift)
            pieces[step] = right
        offsets = sorted(pieces)
        stack = jnp.stack([pieces[o] for o in offsets])
        base = ((1 - 2 * (self.core % 2)) * (self.x - x0)) % nx
        order = []
        for j in range(nx):
            pick = jnp.zeros((), jnp.int32)
            for i, o in enumerate(offsets):
                pick = jnp.where((base + o) % nx == j, i, pick)
            order.append(pick)
        return [pieces[o] for o in offsets], stack, jnp.stack(order)


def solve_panel(factor, blocks):
    count = blocks.shape[0]
    width = blocks.shape[-1]
    stacked = jnp.transpose(blocks, (2, 0, 1)).reshape(width, count * width)
    solved = jax.scipy.linalg.solve_triangular(factor, stacked, lower=True)
    return jnp.transpose(solved.reshape(width, count, width), (1, 2, 0))


def products(rows, far):
    return jnp.einsum("sab,db->sad", rows, far, precision=lax.Precision.HIGHEST)


def make_on_device(shape):
    def on_device(matrix, present, update):
        g = Grid(shape)
        tiles = matrix[:, 0, 0]
        listed = present[:, 0, 0].astype(jnp.float32)
        flags = update[:, :, 0, 0].astype(jnp.float32)
        width = tiles.shape[-1]
        slots = tiles.shape[0]
        n_row, n_col = g.n_row, g.n_col
        identity = jnp.eye(width, dtype=jnp.float32)
        far_slot = g.col // n_row
        far_root = {c: c % n_row for c in range(2, n_col)}

        rows = [(y, k) for y in range(shape[0]) for k in range(shape[1])]
        a_row0, _ = g.send(tiles, [((y, k, 0, 0), (y, k, 0, 1)) for y, k in rows])
        got, hit = g.send(tiles[0], [((0, 0, 0, 0), (0, 0, 0, 1))])
        a00 = g.down_columns(jnp.where(hit, got, tiles[0]), {0: 0, 1: 0})
        a00, a_row0 = lax.optimization_barrier((a00, a_row0))

        owner0 = (g.row == 0) & (g.col == 0)
        second = g.col == 1
        factor0 = jnp.linalg.cholesky(jnp.where((g.col == 0) | second, a00, identity))
        source0 = jnp.where(second, a_row0, tiles)
        p0 = solve_panel(factor0, source0)
        p0 = p0.at[0].set(jnp.where(owner0, factor0, p0[0]))

        head = p0[1 // n_row]
        work11 = tiles[0] - flags[0, 0] * products(head[None], head)[0]
        owner1 = (g.row == 1) & second
        factor1 = jnp.linalg.cholesky(jnp.where(owner1, work11, identity))
        sent = g.down_columns(jnp.stack([factor1, head]), {1: 1 % n_row})
        work1 = tiles - flags[0][:, None, None] * products(p0, sent[1])
        p1 = solve_panel(sent[0], work1)
        p1 = p1.at[0].set(jnp.where(owner1, factor1, p1[0]))
        r01 = p0

        both = jnp.stack([r01, p1], axis=1)
        pieces, stack, order = g.along_rows(both, 1)
        pick = order[far_slot]
        far_in = pieces[0]
        for i in range(1, len(pieces)):
            far_in = jnp.where(pick == i, pieces[i], far_in)
        far = g.down_columns(far_in, far_root)
        rows_both = jnp.take(stack, order, axis=0)
        rest = (tiles - flags[0][:, None, None] * products(rows_both[:, 0], far[0])) - flags[1][
            :, None, None
        ] * products(rows_both[:, 1], far[1])
        out = jnp.where(g.col == 0, p0, jnp.where(g.col == 1, p1, rest))
        return (out * listed[:, None, None])[:, None, None]

    return on_device


def solution(mesh):
    n_row = mesh.shape["row"]
    n_col = mesh.shape["col"]
    shape = (n_row // 2, 2, n_col // 4, 4)
    finer = Mesh(mesh.devices.reshape(shape), AXES)
    return jax.shard_map(
        make_on_device(shape),
        mesh=finer,
        in_specs=(P(None, ROW, COL, None, None), P(None, ROW, COL), P(None, None, ROW, COL)),
        out_specs=P(None, ROW, COL, None, None),
        check_vma=False,
    )
```
